768 devices in a mesh: pipe: 4 (over x), row: 24 (over z, core), col: 8 (over y).
Axes of the slice: x: 4, y: 8, z: 12, core: 2. Of those that a mesh axis runs over, the one named last changes fastest.
Arguments:
- grad_out: bfloat16 [4, 6144, 4608], P('pipe', 'row', 'col'), may hold values from -6 to 6
- out_weight: bfloat16 [4, 2048, 4608], P('pipe', 'col', 'row'), may hold values from -0.09375 to 0.09375
- query_act: bfloat16 [4, 6144, 2048], P('pipe', 'row', 'col'), may hold values from -6 to 6
- key_act: bfloat16 [4, 6144, 1024], P('pipe', 'row', 'col'), may hold values from -18 to 18
- value_act: bfloat16 [4, 6144, 1024], P('pipe', 'row', 'col'), may hold values from -6 to 6
- doc_ids: int32 [4, 6144], P('pipe'), may hold values from 0 to 7, never falling along the last dimension, each value on 1 to 1536 neighbouring positions
- doc_shared: int32 [4, 8], P('pipe'), may hold values 0 or 1
Outputs:
- grad_query: bfloat16 [4, 6144, 2048], P('pipe', 'row', 'col')
- grad_key: bfloat16 [4, 6144, 1024], P('pipe', 'row', 'col')
- grad_value: bfloat16 [4, 6144, 1024], P('pipe', 'row', 'col')
- grad_resid: bfloat16 [4, 6144, 4608], P('pipe', 'row', 'col')
The draws below stay inside these ranges and needn't reach their ends.
Inputs may be any that keep to these rules, and one draw needn't show every extreme that they name: `doc_ids`: never falling along each section's tokens; each document has 1 to 1536 tokens, one exactly 1536.
All inputs are finite; a program needn't handle non-finite values. No bound on the sum of `doc_shared` on one device may be relied on, other than what follows from the above.
Results may differ from the reference program's by a relative error of at most 0.0058.
Values may be sent and summed in bfloat16 or wider, within the bound.
No kernel may reach another device: no remote copies, remote signals or barrier semaphores. Data moves between devices by JAX's collectives and lax.ppermute only.
A program may use at most 32 MiB of HBM per device.

```python
import math
import jax
import jax.numpy as jnp
import numpy as np
from jax import lax

D = 4608
HQ = 16
KVH = 8
HD = 128
WINDOW = 4096
TOK_DEV = 256
NDOC = 8
SEQ = 6144
SECTIONS = 4


def set_ends(values, rng, least, top_value):
    longest = values.shape.index(max(values.shape))
    spots = []
    for shift in (0, 1):
        where = [jax.random.randint(jax.random.fold_in(rng, axis), (), 0, length) for axis, length in enumerate(values.shape)]
        where[longest] = (where[longest] + shift) % values.shape[longest]
        spots.append(tuple(where))
    return values.at[spots[0]].set(least).at[spots[1]].set(top_value)


def block_scale(rng, extent, split, least, top_value):
    gain = 1.0
    for axis_at, parts in split:
        steps = jax.random.uniform(jax.random.fold_in(jax.random.fold_in(rng, 6), axis_at), (parts,), jnp.float32, least / len(split), top_value / len(split))
        gain = gain * jnp.repeat(jnp.exp(steps), extent[axis_at] // parts).reshape((-1,) + (1,) * (len(extent) - 1 - axis_at))
    return gain


def profile(number_of, total, reach, lean):
    portions = [(1 << 20) // math.isqrt(rank ** lean) + 1 for rank in range(2, number_of + 1)]
    surplus, counts = total - reach - (number_of - 1), [1] * (number_of - 1)
    while surplus > 0:
        candidates = [i for i in range(number_of - 1) if counts[i] < reach]
        mass, left = sum([portions[i] for i in candidates]), surplus
        for i in candidates:
            extra = min(reach - counts[i], max(1, left * portions[i] // mass), surplus)
            counts[i] = counts[i] + extra
            surplus = surplus - extra
    return np.array([reach] + counts)


def uneven(key, amount, total, reach, slope):
    if amount == 2:
        one = jax.random.randint(key, (), max(1, total - reach), min(reach, total - 1) + 1)
        return jnp.stack([one, total - one])
    tallies = jnp.asarray(profile(amount, total, reach, slope), jnp.int32)
    pairs = (amount - 1) // 2
    donor, receiver = tallies[1:1 + 2 * pairs:2], tallies[2:2 + 2 * pairs:2]
    room = jnp.minimum(donor - 1, reach - receiver)
    passed = jax.random.randint(jax.random.fold_in(key, 1), (pairs,), 0, 1 << 20) % (room + 1)
    tallies = tallies.at[1:1 + 2 * pairs:2].set(donor - passed).at[2:2 + 2 * pairs:2].set(receiver + passed)
    return tallies[jax.random.permutation(jax.random.fold_in(key, 2), amount)]


def noise(own_key, extent, scale, reach, pieces=(), held_as=jnp.bfloat16):
    array = jax.random.normal(own_key, extent, jnp.float32) * scale
    if len(pieces) > 0:
        array = block_scale(own_key, extent, pieces, -0.22, 0.18) * array
    return jnp.clip(array, min=-reach, max=reach).astype(held_as)


def setup_inputs(seed: int = 0) -> dict:
    key_list = jax.random.split(jax.random.key(seed), 8)
    return {
        "grad_out": noise(key_list[0], (SECTIONS, SEQ, D), 1.0, 6.0, ((0, 4), (1, 24), (2, 8))),
        "out_weight": noise(key_list[1], (SECTIONS, HQ * HD, D), D ** -0.5, 0.09375, ((0, 4), (1, 8), (2, 24))),
        "query_act": noise(key_list[2], (SECTIONS, SEQ, HQ * HD), 1.0, 6.0, ((0, 4), (1, 24), (2, 8))),
        "key_act": noise(key_list[3], (SECTIONS, SEQ, KVH * HD), 3.0, 18.0, ((0, 4), (1, 24), (2, 8))),
        "value_act": noise(key_list[4], (SECTIONS, SEQ, KVH * HD), 1.0, 6.0, ((0, 4), (1, 24), (2, 8))),
        "doc_ids": jax.vmap(lambda own: jnp.searchsorted(jnp.cumsum(uneven(own, NDOC, SEQ, SEQ // 4, 1)), jnp.arange(SEQ), side="right"))(jax.random.split(key_list[5], SECTIONS)).reshape((SECTIONS, SEQ)).astype(jnp.int32),
        "doc_shared": set_ends((jax.random.randint(key_list[6], (SECTIONS, NDOC), 0, 2) < 1).astype(jnp.int32), jax.random.fold_in(key_list[6], 1), 0, 1),
    }


logit_cap = 50.0
score_scale = 144.0 ** -0.5


def section_grads(section_args):
    grad_out, out_weight, query_act, key_act, value_act, doc_row, shared = section_args
    d_attn = jnp.dot(grad_out, out_weight.T, preferred_element_type=jnp.float32).astype(jnp.bfloat16)
    span_rows = WINDOW + TOK_DEV
    block_count = SEQ // TOK_DEV
    key_width = KVH * HD
    doc_row = doc_row.astype(jnp.int32)
    padded_pos = jnp.arange(WINDOW + SEQ, dtype=jnp.int32) - WINDOW
    padded_doc = jnp.concatenate([jnp.full((WINDOW,), -1, jnp.int32), doc_row])
    doc_numbers = jnp.arange(NDOC, dtype=jnp.int32)
    padded_shared = jnp.sum(jnp.where(padded_doc[:, None] == doc_numbers[None, :], shared[None, :], 0), axis=1)
    key_pad = jnp.concatenate([jnp.zeros((WINDOW, key_width), jnp.float32), key_act.astype(jnp.float32)], axis=0)
    value_pad = jnp.concatenate([jnp.zeros((WINDOW, key_width), jnp.float32), value_act.astype(jnp.float32)], axis=0)
    query_full = query_act.astype(jnp.float32)
    attn_full = d_attn.astype(jnp.float32)

    def one_block(running, block_index):
        key_acc, value_acc = running
        block_start = block_index * TOK_DEV
        query_b = lax.dynamic_slice_in_dim(query_full, block_start, TOK_DEV, 0).reshape(TOK_DEV, KVH, 2, HD)
        attn_b = lax.dynamic_slice_in_dim(attn_full, block_start, TOK_DEV, 0).reshape(TOK_DEV, KVH, 2, HD)
        key_b = lax.dynamic_slice_in_dim(key_pad, block_start, span_rows, 0).reshape(span_rows, KVH, HD)
        value_b = lax.dynamic_slice_in_dim(value_pad, block_start, span_rows, 0).reshape(span_rows, KVH, HD)
        key_pos = lax.dynamic_slice_in_dim(padded_pos, block_start, span_rows, 0)
        key_doc = lax.dynamic_slice_in_dim(padded_doc, block_start, span_rows, 0)
        key_shared = lax.dynamic_slice_in_dim(padded_shared, block_start, span_rows, 0)
        query_pos = block_start + jnp.arange(TOK_DEV, dtype=jnp.int32)
        query_doc = lax.dynamic_slice_in_dim(doc_row, block_start, TOK_DEV, 0)
        allowed = (key_pos[None, :] >= 0) & (key_pos[None, :] <= query_pos[:, None]) & (query_pos[:, None] - key_pos[None, :] < WINDOW)
        allowed = allowed & ((key_doc[None, :] == query_doc[:, None]) | (key_shared[None, :] == 1))
        raw_scores = score_scale * jnp.einsum('qgrd,kgd->grqk', query_b, key_b)
        capped = jnp.tanh(raw_scores / logit_cap)
        weights = jnp.where(allowed[None, None], jnp.exp(logit_cap * capped), 0.0)
        attn_probs = weights / jnp.sum(weights, axis=-1, keepdims=True)
        probs_low = lax.optimization_barrier(attn_probs.astype(jnp.bfloat16)).astype(jnp.float32)
        value_part = jnp.einsum('grqk,qgrd->kgd', probs_low, attn_b)
        grad_probs = jnp.einsum('qgrd,kgd->grqk', attn_b, value_b)
        row_delta = jnp.sum(attn_probs * grad_probs, axis=-1, keepdims=True)
        grad_raw = (attn_probs * (grad_probs - row_delta) * (1.0 - capped * capped) * score_scale).astype(jnp.bfloat16)
        grad_raw_f = lax.optimization_barrier(grad_raw).astype(jnp.float32)
        query_grad = jnp.einsum('grqk,kgd->qgrd', grad_raw_f, key_b).astype(jnp.bfloat16).reshape(TOK_DEV, HQ * HD)
        key_part = jnp.einsum('grqk,qgrd->kgd', grad_raw_f, query_b).reshape(span_rows, key_width)
        value_part = value_part.reshape(span_rows, key_width)
        key_acc = lax.dynamic_update_slice_in_dim(key_acc, lax.dynamic_slice_in_dim(key_acc, block_start, span_rows, 0) + key_part, block_start, 0)
        value_acc = lax.dynamic_update_slice_in_dim(value_acc, lax.dynamic_slice_in_dim(value_acc, block_start, span_rows, 0) + value_part, block_start, 0)
        return (key_acc, value_acc), query_grad

    zero_sums = jnp.zeros((WINDOW + SEQ, key_width), jnp.float32)
    (key_acc, value_acc), query_grads = lax.scan(one_block, (zero_sums, zero_sums), jnp.arange(block_count, dtype=jnp.int32))
    query_grad = query_grads.reshape(SEQ, HQ * HD)
    key_grad = key_acc[WINDOW:].astype(jnp.bfloat16)
    value_grad = value_acc[WINDOW:].astype(jnp.bfloat16)
    return query_grad, key_grad, value_grad


def handed_down(stacked):
    return jnp.concatenate([stacked[1:], jnp.zeros_like(stacked[:1])], axis=0)


def reference(grad_out, out_weight, query_act, key_act, value_act, doc_ids, doc_shared):
    query_grad, key_grad, value_grad = lax.map(section_grads, (grad_out, out_weight, query_act, key_act, value_act, doc_ids, doc_shared))
    return (handed_down(query_grad), handed_down(key_grad), handed_down(value_grad), handed_down(grad_out))
```

```python
import jax
import jax.numpy as jnp
from jax import lax
from jax.sharding import PartitionSpec as P

HD = 128
WINDOW = 4096


logit_cap = 50.0
score_scale = 144.0 ** (-0.5)


def from_behind(block, axis, distance):
    devices = range(lax.axis_size(axis))
    route = [(i - distance, i) for i in devices if i - distance in devices]
    return lax.ppermute(block, axis, route)


def attend(query_act, key_near, value_near, d_attn, allowed):
    tok_rows = query_act.shape[0]
    span_rows = key_near.shape[0]
    key_width = key_near.shape[1]
    groups = key_width // HD
    query_heads = jnp.moveaxis(query_act.reshape(tok_rows, 2 * groups, HD), 1, 0)
    attn_heads = jnp.moveaxis(d_attn.reshape(tok_rows, 2 * groups, HD), 1, 0)
    key_heads = jnp.moveaxis(key_near.reshape(span_rows, groups, HD), 1, 0)
    value_heads = jnp.moveaxis(value_near.reshape(span_rows, groups, HD), 1, 0)

    def one_head(running, head_items):
        key_sums, value_sums = running
        head_index, query_h, attn_h = head_items
        group_index = head_index // 2
        key_g = lax.dynamic_index_in_dim(key_heads, group_index, 0, keepdims=False)
        value_g = lax.dynamic_index_in_dim(value_heads, group_index, 0, keepdims=False)
        raw_scores = (
            lax.dot_general(
                query_h, key_g, (((1,), (1,)), ((), ())), preferred_element_type=jnp.float32
            )
            * score_scale
        )
        capped = jnp.tanh(raw_scores / logit_cap)
        weights = jnp.where(allowed, jnp.exp(logit_cap * capped), 0.0)
        attn_probs = weights / jnp.sum(weights, axis=-1, keepdims=True)
        probs_low = attn_probs.astype(jnp.bfloat16)
        value_part = lax.dot_general(
            probs_low, attn_h, (((0,), (0,)), ((), ())), preferred_element_type=jnp.float32
        )
        grad_probs = lax.dot_general(
            attn_h, value_g, (((1,), (1,)), ((), ())), preferred_element_type=jnp.float32
        )
        row_delta = jnp.sum(attn_probs * grad_probs, axis=-1, keepdims=True)
        grad_raw = (
            attn_probs * (grad_probs - row_delta) * (1.0 - capped * capped) * score_scale
        ).astype(jnp.bfloat16)
        query_grad = jnp.dot(grad_raw, key_g, preferred_element_type=jnp.float32).astype(
            jnp.bfloat16
        )
        key_part = lax.dot_general(
            grad_raw, query_h, (((0,), (0,)), ((), ())), preferred_element_type=jnp.float32
        )
        key_sums = lax.dynamic_update_index_in_dim(
            key_sums,
            lax.dynamic_index_in_dim(key_sums, group_index, 0, keepdims=False) + key_part,
            group_index,
            0,
        )
        value_sums = lax.dynamic_update_index_in_dim(
            value_sums,
            lax.dynamic_index_in_dim(value_sums, group_index, 0, keepdims=False) + value_part,
            group_index,
            0,
        )
        return ((key_sums, value_sums), query_grad)

    zero_sums = jnp.zeros((groups, span_rows, HD), jnp.float32)
    head_numbers = jnp.arange(2 * groups, dtype=jnp.int32)
    (key_sums, value_sums), query_grads = lax.scan(
        one_head, (zero_sums, zero_sums), (head_numbers, query_heads, attn_heads)
    )
    query_grad = jnp.moveaxis(query_grads, 0, 1).reshape(tok_rows, 2 * groups * HD)
    key_sum = jnp.moveaxis(key_sums, 0, 1).reshape(span_rows, key_width)
    value_sum = jnp.moveaxis(value_sums, 0, 1).reshape(span_rows, key_width)
    return (query_grad, key_sum, value_sum)


def shared_lookup(key_doc, shared_flags):
    doc_numbers = jnp.arange(shared_flags.shape[0], dtype=jnp.int32)
    return jnp.sum(
        jnp.where(key_doc[:, None] == doc_numbers[None, :], shared_flags[None, :], 0), axis=1
    )


def per_device(grad_out, out_weight, query_act, key_act, value_act, doc_ids, doc_shared):
    grad_tile = grad_out[0]
    tok_rows = grad_tile.shape[0]
    grad_rows = lax.all_gather(grad_tile, "col", axis=1, tiled=True)
    d_attn = lax.dot_general(
        grad_rows,
        lax.all_gather(out_weight[0], "row", axis=1, tiled=True),
        (((1,), (1,)), ((), ())),
        preferred_element_type=jnp.float32,
    ).astype(jnp.bfloat16)
    reach_rows = min(lax.axis_size("row") - 1, WINDOW // tok_rows)
    span_rows = (reach_rows + 1) * tok_rows
    row_index = lax.axis_index("row")
    query_start = row_index * tok_rows
    doc_list = doc_ids[0]
    shared_flags = doc_shared[0]
    query_local = query_act[0]
    key_local = key_act[0]
    value_local = value_act[0]
    key_width = key_local.shape[1]
    pair_local = jnp.concatenate([key_local, value_local], axis=1)
    near_blocks = [pair_local]
    moving = pair_local
    for _ in range(reach_rows):
        moving = from_behind(moving, "row", 1)
        near_blocks.append(moving)
    pair_near = jnp.concatenate(near_blocks[::-1], axis=0)
    key_near = pair_near[:, :key_width]
    value_near = pair_near[:, key_width:]
    key_start = query_start - reach_rows * tok_rows
    key_pos = key_start + jnp.arange(span_rows, dtype=jnp.int32)
    query_pos = query_start + jnp.arange(tok_rows, dtype=jnp.int32)
    query_doc = lax.dynamic_slice_in_dim(doc_list, query_start, tok_rows)
    padded_docs = jnp.concatenate([jnp.full((reach_rows * tok_rows,), -1, jnp.int32), doc_list])
    key_doc = lax.dynamic_slice_in_dim(padded_docs, query_start, span_rows)
    key_shared = shared_lookup(key_doc, shared_flags)
    allowed = (
        (key_pos[None, :] >= 0)
        & (key_pos[None, :] <= query_pos[:, None])
        & (query_pos[:, None] - key_pos[None, :] < WINDOW)
    )
    allowed = allowed & ((key_doc[None, :] == query_doc[:, None]) | (key_shared[None, :] == 1))
    query_grad, key_sum, value_sum = attend(query_local, key_near, value_near, d_attn, allowed)
    pair_sum = jnp.concatenate([key_sum, value_sum], axis=1)
    running = pair_sum[:tok_rows]
    for step in range(1, reach_rows + 1):
        running = from_behind(running, "row", -1) + pair_sum[step * tok_rows : (step + 1) * tok_rows]
    key_total = running[:, :key_width]
    value_total = running[:, key_width:]
    handed = from_behind(
        (query_grad, key_total.astype(jnp.bfloat16), value_total.astype(jnp.bfloat16), grad_tile),
        "pipe",
        -1,
    )
    return (handed[0][None], handed[1][None], handed[2][None], handed[3][None])


def solution(mesh):
    in_specs = (
        P("pipe", "row", "col"),
        P("pipe", "col", "row"),
        P("pipe", "row", "col"),
        P("pipe", "row", "col"),
        P("pipe", "row", "col"),
        P("pipe", None),
        P("pipe", None),
    )
    out_specs = (
        P("pipe", "row", "col"),
        P("pipe", "row", "col"),
        P("pipe", "row", "col"),
        P("pipe", "row", "col"),
    )
    return jax.shard_map(
        per_device, mesh=mesh, in_specs=in_specs, out_specs=out_specs, check_vma=False
    )
```

```python
import jax
import jax.numpy as jnp
from jax import lax
from jax.sharding import PartitionSpec as P

HD = 128
WINDOW = 4096


logit_cap = 50.0
score_scale = 144.0 ** (-0.5)


def from_behind(block, axis, distance):
    devices = range(lax.axis_size(axis))
    route = [(i - distance, i) for i in devices if i - distance in devices]
    return lax.ppermute(block, axis, route)


def attend(query_act, key_near, value_near, d_attn, allowed):
    tok_rows = query_act.shape[0]
    span_rows = key_near.shape[0]
    key_width = key_near.shape[1]
    groups = key_width // HD
    query_heads = jnp.moveaxis(query_act.reshape(tok_rows, 2 * groups, HD), 1, 0)
    attn_heads = jnp.moveaxis(d_attn.reshape(tok_rows, 2 * groups, HD), 1, 0)
    key_heads = jnp.moveaxis(key_near.reshape(span_rows, groups, HD), 1, 0)
    value_heads = jnp.moveaxis(value_near.reshape(span_rows, groups, HD), 1, 0)

    def one_head(running, head_items):
        key_sums, value_sums = running
        head_index, query_h, attn_h = head_items
        group_index = head_index // 2
        key_g = lax.dynamic_index_in_dim(key_heads, group_index, 0, keepdims=False)
        value_g = lax.dynamic_index_in_dim(value_heads, group_index, 0, keepdims=False)
        raw_scores = (
            lax.dot_general(
                query_h, key_g, (((1,), (1,)), ((), ())), preferred_element_type=jnp.float32
            )
            * score_scale
        )
        capped = jnp.tanh(raw_scores / logit_cap)
        weights = jnp.where(allowed, jnp.exp(logit_cap * capped), 0.0)
        attn_probs = weights / jnp.sum(weights, axis=-1, keepdims=True)
        probs_low = attn_probs.astype(jnp.bfloat16)
        value_part = lax.dot_general(
            probs_low, attn_h, (((0,), (0,)), ((), ())), preferred_element_type=jnp.float32
        )
        grad_probs = lax.dot_general(
            attn_h, value_g, (((1,), (1,)), ((), ())), preferred_element_type=jnp.float32
        )
        row_delta = jnp.sum(attn_probs * grad_probs, axis=-1, keepdims=True)
        grad_raw = (
            attn_probs * (grad_probs - row_delta) * (1.0 - capped * capped) * score_scale
        ).astype(jnp.bfloat16)
        query_grad = jnp.dot(grad_raw, key_g, preferred_element_type=jnp.float32).astype(
            jnp.bfloat16
        )
        key_part = lax.dot_general(
            grad_raw, query_h, (((0,), (0,)), ((), ())), preferred_element_type=jnp.float32
        )
        key_sums = lax.dynamic_update_index_in_dim(
            key_sums,
            lax.dynamic_index_in_dim(key_sums, group_index, 0, keepdims=False) + key_part,
            group_index,
            0,
        )
        value_sums = lax.dynamic_update_index_in_dim(
            value_sums,
            lax.dynamic_index_in_dim(value_sums, group_index, 0, keepdims=False) + value_part,
            group_index,
            0,
        )
        return ((key_sums, value_sums), query_grad)

    zero_sums = jnp.zeros((groups, span_rows, HD), jnp.float32)
    head_numbers = jnp.arange(2 * groups, dtype=jnp.int32)
    (key_sums, value_sums), query_grads = lax.scan(
        one_head, (zero_sums, zero_sums), (head_numbers, query_heads, attn_heads)
    )
    query_grad = jnp.moveaxis(query_grads, 0, 1).reshape(tok_rows, 2 * groups * HD)
    key_sum = jnp.moveaxis(key_sums, 0, 1).reshape(span_rows, key_width)
    value_sum = jnp.moveaxis(value_sums, 0, 1).reshape(span_rows, key_width)
    return (query_grad, key_sum, value_sum)


def shared_lookup(key_doc, shared_flags):
    doc_numbers = jnp.arange(shared_flags.shape[0], dtype=jnp.int32)
    return jnp.sum(
        jnp.where(key_doc[:, None] == doc_numbers[None, :], shared_flags[None, :], 0), axis=1
    )


def per_device(grad_out, out_weight, query_act, key_act, value_act, doc_ids, doc_shared):
    grad_tile = grad_out[0]
    tok_rows = grad_tile.shape[0]
    grad_rows = lax.all_gather(grad_tile, "col", axis=1, tiled=True)
    d_attn = lax.dot_general(
        grad_rows,
        lax.all_gather(out_weight[0], "row", axis=1, tiled=True),
        (((1,), (1,)), ((), ())),
        preferred_element_type=jnp.float32,
    ).astype(jnp.bfloat16)
    reach_rows = min(lax.axis_size("row") - 1, WINDOW // tok_rows)
    span_rows = (reach_rows + 1) * tok_rows
    row_index = lax.axis_index("row")
    query_start = row_index * tok_rows
    doc_list = doc_ids[0]
    shared_flags = doc_shared[0]
    query_local = query_act[0]
    key_local = key_act[0]
    value_local = value_act[0]
    key_width = key_local.shape[1]
    pair_local = jnp.concatenate([key_local, value_local], axis=1)
    near_blocks = [pair_local]
    moving = pair_local
    for _ in range(reach_rows):
        moving = from_behind(moving, "row", 1)
        near_blocks.append(moving)
    pair_near = jnp.concatenate(near_blocks[::-1], axis=0)
    key_near = pair_near[:, :key_width]
    value_near = pair_near[:, key_width:]
    key_start = query_start - reach_rows * tok_rows
    key_pos = key_start + jnp.arange(span_rows, dtype=jnp.int32)
    query_pos = query_start + jnp.arange(tok_rows, dtype=jnp.int32)
    query_doc = lax.dynamic_slice_in_dim(doc_list, query_start, tok_rows)
    padded_docs = jnp.concatenate([jnp.full((reach_rows * tok_rows,), -1, jnp.int32), doc_list])
    key_doc = lax.dynamic_slice_in_dim(padded_docs, query_start, span_rows)
    key_shared = shared_lookup(key_doc, shared_flags)
    allowed = (
        (key_pos[None, :] >= 0)
        & (key_pos[None, :] <= query_pos[:, None])
        & (query_pos[:, None] - key_pos[None, :] < WINDOW)
    )
    allowed = allowed & ((key_doc[None, :] == query_doc[:, None]) | (key_shared[None, :] == 1))
    query_grad, key_sum, value_sum = attend(query_local, key_near, value_near, d_attn, allowed)
    pair_sum = jnp.concatenate([key_sum, value_sum], axis=1)
    pair_sum = pair_sum.reshape(reach_rows + 1, tok_rows, 2 * key_width)
    even_part = pair_sum[0::2]
    odd_part = pair_sum[1::2]
    partner = lax.ppermute(
        odd_part, "row", [(i, i ^ 1) for i in range(lax.axis_size("row"))]
    )
    core_bit = row_index % 2
    zero_block = jnp.zeros_like(odd_part[:1])
    partner_aligned = jnp.where(
        core_bit == 0,
        jnp.concatenate([zero_block, partner], axis=0),
        jnp.concatenate([partner, zero_block], axis=0),
    )
    chip_sum = even_part + partner_aligned
    running = chip_sum[0]
    for step in range(1, reach_rows // 2 + 1):
        running = from_behind(running, "row", -2) + chip_sum[step]
    key_total = running[:, :key_width]
    value_total = running[:, key_width:]
    handed = from_behind(
        (query_grad, key_total.astype(jnp.bfloat16), value_total.astype(jnp.bfloat16), grad_tile),
        "pipe",
        -1,
    )
    return (handed[0][None], handed[1][None], handed[2][None], handed[3][None])


def solution(mesh):
    in_specs = (
        P("pipe", "row", "col"),
        P("pipe", "col", "row"),
        P("pipe", "row", "col"),
        P("pipe", "row", "col"),
        P("pipe", "row", "col"),
        P("pipe", None),
        P("pipe", None),
    )
    out_specs = (
        P("pipe", "row", "col"),
        P("pipe", "row", "col"),
        P("pipe", "row", "col"),
        P("pipe", "row", "col"),
    )
    return jax.shard_map(
        per_device, mesh=mesh, in_specs=in_specs, out_specs=out_specs, check_vma=False
    )
```

```python
import jax
import jax.numpy as jnp
from jax import lax
from jax.sharding import PartitionSpec as P

HD = 128
WINDOW = 4096


logit_cap = 50.0
score_scale = 144.0 ** (-0.5)


def from_behind(block, axis, distance):
    devices = range(lax.axis_size(axis))
    route = [(i - distance, i) for i in devices if i - distance in devices]
    return lax.ppermute(block, axis, route)


def cyclic_shift(block, axis, distance):
    size = lax.axis_size(axis)
    return lax.ppermute(block, axis, [(i, (i + distance) % size) for i in range(size)])


def ring_gather(block, axis):
    size = lax.axis_size(axis)
    ahead = [block]
    behind = []
    forward = block
    backward = block
    for _ in range(size // 2):
        forward = cyclic_shift(forward, axis, 1)
        behind.append(forward)
    for _ in range((size - 1) // 2):
        backward = cyclic_shift(backward, axis, -1)
        ahead.append(backward)
    relative = jnp.stack(ahead + behind[::-1], axis=0)
    rolled = jnp.roll(relative, lax.axis_index(axis), axis=0)
    return jnp.moveaxis(rolled, 0, 1).reshape(block.shape[0], size * block.shape[1])


def attend(query_act, key_near, value_near, d_attn, allowed):
    tok_rows = query_act.shape[0]
    span_rows = key_near.shape[0]
    key_width = key_near.shape[1]
    groups = key_width // HD
    query_heads = jnp.moveaxis(query_act.reshape(tok_rows, 2 * groups, HD), 1, 0)
    attn_heads = jnp.moveaxis(d_attn.reshape(tok_rows, 2 * groups, HD), 1, 0)
    key_heads = jnp.moveaxis(key_near.reshape(span_rows, groups, HD), 1, 0)
    value_heads = jnp.moveaxis(value_near.reshape(span_rows, groups, HD), 1, 0)

    def one_head(running, head_items):
        key_sums, value_sums = running
        head_index, query_h, attn_h = head_items
        group_index = head_index // 2
        key_g = lax.dynamic_index_in_dim(key_heads, group_index, 0, keepdims=False)
        value_g = lax.dynamic_index_in_dim(value_heads, group_index, 0, keepdims=False)
        raw_scores = (
            lax.dot_general(
                query_h, key_g, (((1,), (1,)), ((), ())), preferred_element_type=jnp.float32
            )
            * score_scale
        )
        capped = jnp.tanh(raw_scores / logit_cap)
        weights = jnp.where(allowed, jnp.exp(logit_cap * capped), 0.0)
        attn_probs = weights / jnp.sum(weights, axis=-1, keepdims=True)
        probs_low = attn_probs.astype(jnp.bfloat16)
        value_part = lax.dot_general(
            probs_low, attn_h, (((0,), (0,)), ((), ())), preferred_element_type=jnp.float32
        )
        grad_probs = lax.dot_general(
            attn_h, value_g, (((1,), (1,)), ((), ())), preferred_element_type=jnp.float32
        )
        row_delta = jnp.sum(attn_probs * grad_probs, axis=-1, keepdims=True)
        grad_raw = (
            attn_probs * (grad_probs - row_delta) * (1.0 - capped * capped) * score_scale
        ).astype(jnp.bfloat16)
        query_grad = jnp.dot(grad_raw, key_g, preferred_element_type=jnp.float32).astype(
            jnp.bfloat16
        )
        key_part = lax.dot_general(
            grad_raw, query_h, (((0,), (0,)), ((), ())), preferred_element_type=jnp.float32
        )
        key_sums = lax.dynamic_update_index_in_dim(
            key_sums,
            lax.dynamic_index_in_dim(key_sums, group_index, 0, keepdims=False) + key_part,
            group_index,
            0,
        )
        value_sums = lax.dynamic_update_index_in_dim(
            value_sums,
            lax.dynamic_index_in_dim(value_sums, group_index, 0, keepdims=False) + value_part,
            group_index,
            0,
        )
        return ((key_sums, value_sums), query_grad)

    zero_sums = jnp.zeros((groups, span_rows, HD), jnp.float32)
    head_numbers = jnp.arange(2 * groups, dtype=jnp.int32)
    (key_sums, value_sums), query_grads = lax.scan(
        one_head, (zero_sums, zero_sums), (head_numbers, query_heads, attn_heads)
    )
    query_grad = jnp.moveaxis(query_grads, 0, 1).reshape(tok_rows, 2 * groups * HD)
    key_sum = jnp.moveaxis(key_sums, 0, 1).reshape(span_rows, key_width)
    value_sum = jnp.moveaxis(value_sums, 0, 1).reshape(span_rows, key_width)
    return (query_grad, key_sum, value_sum)


def shared_lookup(key_doc, shared_flags):
    doc_numbers = jnp.arange(shared_flags.shape[0], dtype=jnp.int32)
    return jnp.sum(
        jnp.where(key_doc[:, None] == doc_numbers[None, :], shared_flags[None, :], 0), axis=1
    )


def per_device(grad_out, out_weight, query_act, key_act, value_act, doc_ids, doc_shared):
    grad_tile = grad_out[0]
    tok_rows = grad_tile.shape[0]
    grad_rows = ring_gather(grad_tile, "col")
    d_attn = lax.dot_general(
        grad_rows,
        lax.all_gather(out_weight[0], "row", axis=1, tiled=True),
        (((1,), (1,)), ((), ())),
        preferred_element_type=jnp.float32,
    ).astype(jnp.bfloat16)
    reach_rows = min(lax.axis_size("row") - 1, WINDOW // tok_rows)
    span_rows = (reach_rows + 1) * tok_rows
    row_index = lax.axis_index("row")
    query_start = row_index * tok_rows
    doc_list = doc_ids[0]
    shared_flags = doc_shared[0]
    query_local = query_act[0]
    key_local = key_act[0]
    value_local = value_act[0]
    key_width = key_local.shape[1]
    pair_local = jnp.concatenate([key_local, value_local], axis=1)
    core_bit = row_index % 2
    pair_partner = lax.ppermute(
        pair_local, "row", [(i, i ^ 1) for i in range(lax.axis_size("row"))]
    )
    moving = jnp.where(
        core_bit == 0,
        jnp.concatenate([pair_local, pair_partner], axis=0),
        jnp.concatenate([pair_partner, pair_local], axis=0),
    )
    near_blocks = [moving]
    for _ in range(reach_rows // 2):
        moving = from_behind(moving, "row", 2)
        near_blocks.append(moving)
    pair_near = lax.dynamic_slice_in_dim(
        jnp.concatenate(near_blocks[::-1], axis=0), core_bit * tok_rows, span_rows, 0
    )
    key_near = pair_near[:, :key_width]
    value_near = pair_near[:, key_width:]
    key_start = query_start - reach_rows * tok_rows
    key_pos = key_start + jnp.arange(span_rows, dtype=jnp.int32)
    query_pos = query_start + jnp.arange(tok_rows, dtype=jnp.int32)
    query_doc = lax.dynamic_slice_in_dim(doc_list, query_start, tok_rows)
    padded_docs = jnp.concatenate([jnp.full((reach_rows * tok_rows,), -1, jnp.int32), doc_list])
    key_doc = lax.dynamic_slice_in_dim(padded_docs, query_start, span_rows)
    key_shared = shared_lookup(key_doc, shared_flags)
    allowed = (
        (key_pos[None, :] >= 0)
        & (key_pos[None, :] <= query_pos[:, None])
        & (query_pos[:, None] - key_pos[None, :] < WINDOW)
    )
    allowed = allowed & ((key_doc[None, :] == query_doc[:, None]) | (key_shared[None, :] == 1))
    query_grad, key_sum, value_sum = attend(query_local, key_near, value_near, d_attn, allowed)
    pair_sum = jnp.concatenate([key_sum, value_sum], axis=1)
    pair_sum = pair_sum.reshape(reach_rows + 1, tok_rows, 2 * key_width)
    even_part = pair_sum[0::2]
    odd_part = pair_sum[1::2]
    partner = lax.ppermute(
        odd_part, "row", [(i, i ^ 1) for i in range(lax.axis_size("row"))]
    )
    zero_block = jnp.zeros_like(odd_part[:1])
    partner_aligned = jnp.where(
        core_bit == 0,
        jnp.concatenate([zero_block, partner], axis=0),
        jnp.concatenate([partner, zero_block], axis=0),
    )
    chip_sum = even_part + partner_aligned
    running = chip_sum[0]
    for step in range(1, reach_rows // 2 + 1):
        running = from_behind(running, "row", -2) + chip_sum[step]
    key_total = running[:, :key_width]
    value_total = running[:, key_width:]
    handed = from_behind(
        (query_grad, key_total.astype(jnp.bfloat16), value_total.astype(jnp.bfloat16), grad_tile),
        "pipe",
        -1,
    )
    return (handed[0][None], handed[1][None], handed[2][None], handed[3][None])


def solution(mesh):
    in_specs = (
        P("pipe", "row", "col"),
        P("pipe", "col", "row"),
        P("pipe", "row", "col"),
        P("pipe", "row", "col"),
        P("pipe", "row", "col"),
        P("pipe", None),
        P("pipe", None),
    )
    out_specs = (
        P("pipe", "row", "col"),
        P("pipe", "row", "col"),
        P("pipe", "row", "col"),
        P("pipe", "row", "col"),
    )
    return jax.shard_map(
        per_device, mesh=mesh, in_specs=in_specs, out_specs=out_specs, check_vma=False
    )
```

```python
import jax
import jax.numpy as jnp
from jax import lax
from jax.sharding import PartitionSpec as P

HD = 128
WINDOW = 4096


logit_cap = 50.0
score_scale = 144.0 ** (-0.5)


def from_behind(block, axis, distance):
    devices = range(lax.axis_size(axis))
    route = [(i - distance, i) for i in devices if i - distance in devices]
    return lax.ppermute(block, axis, route)


def cyclic_shift(block, axis, distance):
    size = lax.axis_size(axis)
    return lax.ppermute(block, axis, [(i, (i + distance) % size) for i in range(size)])


def ring_gather(block, axis):
    size = lax.axis_size(axis)
    ahead = [block]
    behind = []
    forward = block
    backward = block
    for _ in range(size // 2):
        forward = cyclic_shift(forward, axis, 1)
        behind.append(forward)
    for _ in range((size - 1) // 2):
        backward = cyclic_shift(backward, axis, -1)
        ahead.append(backward)
    relative = jnp.stack(ahead + behind[::-1], axis=0)
    rolled = jnp.roll(relative, lax.axis_index(axis), axis=0)
    return jnp.moveaxis(rolled, 0, 1).reshape(block.shape[0], size * block.shape[1])


def attend(query_act, key_near, value_near, d_attn, allowed):
    tok_rows = query_act.shape[0]
    span_rows = key_near.shape[0]
    key_width = key_near.shape[1]
    groups = key_width // HD
    query_heads = jnp.moveaxis(query_act.reshape(tok_rows, 2 * groups, HD), 1, 0)
    attn_heads = jnp.moveaxis(d_attn.reshape(tok_rows, 2 * groups, HD), 1, 0)
    key_heads = jnp.moveaxis(key_near.reshape(span_rows, groups, HD), 1, 0)
    value_heads = jnp.moveaxis(value_near.reshape(span_rows, groups, HD), 1, 0)

    def one_head(running, head_items):
        key_sums, value_sums = running
        head_index, query_h, attn_h = head_items
        group_index = head_index // 2
        key_g = lax.dynamic_index_in_dim(key_heads, group_index, 0, keepdims=False)
        value_g = lax.dynamic_index_in_dim(value_heads, group_index, 0, keepdims=False)
        raw_scores = (
            lax.dot_general(
                query_h, key_g, (((1,), (1,)), ((), ())), preferred_element_type=jnp.float32
            )
            * score_scale
        )
        capped = jnp.tanh(raw_scores / logit_cap)
        weights = jnp.where(allowed, jnp.exp(logit_cap * capped), 0.0)
        attn_probs = weights / jnp.sum(weights, axis=-1, keepdims=True)
        probs_low = attn_probs.astype(jnp.bfloat16)
        value_part = lax.dot_general(
            probs_low, attn_h, (((0,), (0,)), ((), ())), preferred_element_type=jnp.float32
        )
        grad_probs = lax.dot_general(
            attn_h, value_g, (((1,), (1,)), ((), ())), preferred_element_type=jnp.float32
        )
        row_delta = jnp.sum(attn_probs * grad_probs, axis=-1, keepdims=True)
        grad_raw = (
            attn_probs * (grad_probs - row_delta) * (1.0 - capped * capped) * score_scale
        ).astype(jnp.bfloat16)
        query_grad = jnp.dot(grad_raw, key_g, preferred_element_type=jnp.float32).astype(
            jnp.bfloat16
        )
        key_part = lax.dot_general(
            grad_raw, query_h, (((0,), (0,)), ((), ())), preferred_element_type=jnp.float32
        )
        key_sums = lax.dynamic_update_index_in_dim(
            key_sums,
            lax.dynamic_index_in_dim(key_sums, group_index, 0, keepdims=False) + key_part,
            group_index,
            0,
        )
        value_sums = lax.dynamic_update_index_in_dim(
            value_sums,
            lax.dynamic_index_in_dim(value_sums, group_index, 0, keepdims=False) + value_part,
            group_index,
            0,
        )
        return ((key_sums, value_sums), query_grad)

    zero_sums = jnp.zeros((groups, span_rows, HD), jnp.float32)
    head_numbers = jnp.arange(2 * groups, dtype=jnp.int32)
    (key_sums, value_sums), query_grads = lax.scan(
        one_head, (zero_sums, zero_sums), (head_numbers, query_heads, attn_heads)
    )
    query_grad = jnp.moveaxis(query_grads, 0, 1).reshape(tok_rows, 2 * groups * HD)
    key_sum = jnp.moveaxis(key_sums, 0, 1).reshape(span_rows, key_width)
    value_sum = jnp.moveaxis(value_sums, 0, 1).reshape(span_rows, key_width)
    return (query_grad, key_sum, value_sum)


def shared_lookup(key_doc, shared_flags):
    doc_numbers = jnp.arange(shared_flags.shape[0], dtype=jnp.int32)
    return jnp.sum(
        jnp.where(key_doc[:, None] == doc_numbers[None, :], shared_flags[None, :], 0), axis=1
    )


def per_device(grad_out, out_weight, query_act, key_act, value_act, doc_ids, doc_shared):
    grad_tile = grad_out[0]
    tok_rows = grad_tile.shape[0]
    grad_rows = ring_gather(grad_tile, "col")
    d_attn = lax.dot_general(
        grad_rows,
        lax.all_gather(out_weight[0], "row", axis=1, tiled=True),
        (((1,), (1,)), ((), ())),
        preferred_element_type=jnp.float32,
    ).astype(jnp.bfloat16)
    reach_rows = min(lax.axis_size("row") - 1, WINDOW // tok_rows)
    span_rows = (reach_rows + 1) * tok_rows
    row_index = lax.axis_index("row")
    query_start = row_index * tok_rows
    doc_list = doc_ids[0]
    shared_flags = doc_shared[0]
    query_local = query_act[0]
    key_local = key_act[0]
    value_local = value_act[0]
    key_width = key_local.shape[1]
    pair_local = jnp.concatenate([key_local, value_local], axis=1)
    core_bit = row_index % 2
    moving = pair_local
    same_core = []
    for _ in range(reach_rows // 2):
        moving = from_behind(moving, "row", 2)
        same_core.append(moving)
    same_core = jnp.stack([pair_local] + same_core, axis=0)
    other_core = lax.ppermute(
        same_core, "row", [(i, i ^ 1) for i in range(lax.axis_size("row"))]
    )
    pairs = jnp.where(
        core_bit == 0,
        jnp.stack([same_core, other_core], axis=1),
        jnp.stack([other_core, same_core], axis=1),
    )
    pair_near = lax.dynamic_slice_in_dim(
        pairs[::-1].reshape(-1, pair_local.shape[1]), core_bit * tok_rows, span_rows, 0
    )
    key_near = pair_near[:, :key_width]
    value_near = pair_near[:, key_width:]
    key_start = query_start - reach_rows * tok_rows
    key_pos = key_start + jnp.arange(span_rows, dtype=jnp.int32)
    query_pos = query_start + jnp.arange(tok_rows, dtype=jnp.int32)
    query_doc = lax.dynamic_slice_in_dim(doc_list, query_start, tok_rows)
    padded_docs = jnp.concatenate([jnp.full((reach_rows * tok_rows,), -1, jnp.int32), doc_list])
    key_doc = lax.dynamic_slice_in_dim(padded_docs, query_start, span_rows)
    key_shared = shared_lookup(key_doc, shared_flags)
    allowed = (
        (key_pos[None, :] >= 0)
        & (key_pos[None, :] <= query_pos[:, None])
        & (query_pos[:, None] - key_pos[None, :] < WINDOW)
    )
    allowed = allowed & ((key_doc[None, :] == query_doc[:, None]) | (key_shared[None, :] == 1))
    query_grad, key_sum, value_sum = attend(query_local, key_near, value_near, d_attn, allowed)
    pair_sum = jnp.concatenate([key_sum, value_sum], axis=1)
    pair_sum = pair_sum.reshape(reach_rows + 1, tok_rows, 2 * key_width)
    even_part = pair_sum[0::2]
    odd_part = pair_sum[1::2]
    partner = lax.ppermute(
        odd_part, "row", [(i, i ^ 1) for i in range(lax.axis_size("row"))]
    )
    zero_block = jnp.zeros_like(odd_part[:1])
    partner_aligned = jnp.where(
        core_bit == 0,
        jnp.concatenate([zero_block, partner], axis=0),
        jnp.concatenate([partner, zero_block], axis=0),
    )
    chip_sum = even_part + partner_aligned
    running = chip_sum[0]
    for step in range(1, reach_rows // 2 + 1):
        running = from_behind(running, "row", -2) + chip_sum[step]
    key_total = running[:, :key_width]
    value_total = running[:, key_width:]
    handed = from_behind(
        (query_grad, key_total.astype(jnp.bfloat16), value_total.astype(jnp.bfloat16), grad_tile),
        "pipe",
        -1,
    )
    return (handed[0][None], handed[1][None], handed[2][None], handed[3][None])


def solution(mesh):
    in_specs = (
        P("pipe", "row", "col"),
        P("pipe", "col", "row"),
        P("pipe", "row", "col"),
        P("pipe", "row", "col"),
        P("pipe", "row", "col"),
        P("pipe", None),
        P("pipe", None),
    )
    out_specs = (
        P("pipe", "row", "col"),
        P("pipe", "row", "col"),
        P("pipe", "row", "col"),
        P("pipe", "row", "col"),
    )
    return jax.shard_map(
        per_device, mesh=mesh, in_specs=in_specs, out_specs=out_specs, check_vma=False
    )
```

```python
import jax
import jax.numpy as jnp
from jax import lax
from jax.sharding import PartitionSpec as P

HD = 128
WINDOW = 4096


logit_cap = 50.0
score_scale = 144.0 ** (-0.5)


def from_behind(block, axis, distance):
    devices = range(lax.axis_size(axis))
    route = [(i - distance, i) for i in devices if i - distance in devices]
    return lax.ppermute(block, axis, route)


def cyclic_shift(block, axis, distance):
    size = lax.axis_size(axis)
    return lax.ppermute(block, axis, [(i, (i + distance) % size) for i in range(size)])


def ring_gather(block, axis):
    size = lax.axis_size(axis)
    ahead = [block]
    behind = []
    forward = block
    backward = block
    for _ in range(size // 2):
        forward = cyclic_shift(forward, axis, 1)
        behind.append(forward)
    for _ in range((size - 1) // 2):
        backward = cyclic_shift(backward, axis, -1)
        ahead.append(backward)
    relative = jnp.stack(ahead + behind[::-1], axis=0)
    rolled = jnp.roll(relative, lax.axis_index(axis), axis=0)
    return jnp.moveaxis(rolled, 0, 1).reshape(block.shape[0], size * block.shape[1])


def attend(query_act, key_near, value_near, d_attn, allowed):
    tok_rows = query_act.shape[0]
    span_rows = key_near.shape[0]
    key_width = key_near.shape[1]
    groups = key_width // HD
    query_g = query_act.reshape(tok_rows, groups, 2, HD)
    attn_g = d_attn.reshape(tok_rows, groups, 2, HD)
    key_g = key_near.reshape(span_rows, groups, HD)
    value_g = value_near.reshape(span_rows, groups, HD)
    raw_scores = (
        jnp.einsum("qgrd,kgd->grqk", query_g, key_g, preferred_element_type=jnp.float32)
        * score_scale
    )
    capped = jnp.tanh(raw_scores / logit_cap)
    weights = jnp.where(allowed[None, None], jnp.exp(logit_cap * capped), 0.0)
    attn_probs = weights / jnp.sum(weights, axis=-1, keepdims=True)
    probs_low = attn_probs.astype(jnp.bfloat16)
    value_sum = jnp.einsum(
        "grqk,qgrd->kgd", probs_low, attn_g, preferred_element_type=jnp.float32
    )
    grad_probs = jnp.einsum(
        "qgrd,kgd->grqk", attn_g, value_g, preferred_element_type=jnp.float32
    )
    row_delta = jnp.sum(attn_probs * grad_probs, axis=-1, keepdims=True)
    grad_raw = (
        attn_probs * (grad_probs - row_delta) * (1.0 - capped * capped) * score_scale
    ).astype(jnp.bfloat16)
    query_grad = jnp.einsum(
        "grqk,kgd->qgrd", grad_raw, key_g, preferred_element_type=jnp.float32
    ).astype(jnp.bfloat16)
    key_sum = jnp.einsum(
        "grqk,qgrd->kgd", grad_raw, query_g, preferred_element_type=jnp.float32
    )
    return (
        query_grad.reshape(tok_rows, key_width * 2),
        key_sum.reshape(span_rows, key_width),
        value_sum.reshape(span_rows, key_width),
    )


def shared_lookup(key_doc, shared_flags):
    doc_numbers = jnp.arange(shared_flags.shape[0], dtype=jnp.int32)
    return jnp.sum(
        jnp.where(key_doc[:, None] == doc_numbers[None, :], shared_flags[None, :], 0), axis=1
    )


def per_device(grad_out, out_weight, query_act, key_act, value_act, doc_ids, doc_shared):
    grad_tile = grad_out[0]
    tok_rows = grad_tile.shape[0]
    grad_handed = from_behind(grad_tile, "pipe", -1)
    grad_rows = ring_gather(grad_tile, "col")
    d_attn = lax.dot_general(
        grad_rows,
        lax.all_gather(out_weight[0], "row", axis=1, tiled=True),
        (((1,), (1,)), ((), ())),
        preferred_element_type=jnp.float32,
    ).astype(jnp.bfloat16)
    reach_rows = min(lax.axis_size("row") - 1, WINDOW // tok_rows)
    span_rows = (reach_rows + 1) * tok_rows
    row_index = lax.axis_index("row")
    query_start = row_index * tok_rows
    doc_list = doc_ids[0]
    shared_flags = doc_shared[0]
    query_local = query_act[0]
    key_local = key_act[0]
    value_local = value_act[0]
    key_width = key_local.shape[1]
    pair_local = jnp.concatenate([key_local, value_local], axis=1)
    core_bit = row_index % 2
    moving = pair_local
    same_core = []
    for _ in range(reach_rows // 2):
        moving = from_behind(moving, "row", 2)
        same_core.append(moving)
    same_core = jnp.stack([pair_local] + same_core, axis=0)
    other_core = lax.ppermute(
        same_core, "row", [(i, i ^ 1) for i in range(lax.axis_size("row"))]
    )
    pairs = jnp.where(
        core_bit == 0,
        jnp.stack([same_core, other_core], axis=1),
        jnp.stack([other_core, same_core], axis=1),
    )
    pair_near = lax.dynamic_slice_in_dim(
        pairs[::-1].reshape(-1, pair_local.shape[1]), core_bit * tok_rows, span_rows, 0
    )
    key_near = pair_near[:, :key_width]
    value_near = pair_near[:, key_width:]
    key_start = query_start - reach_rows * tok_rows
    key_pos = key_start + jnp.arange(span_rows, dtype=jnp.int32)
    query_pos = query_start + jnp.arange(tok_rows, dtype=jnp.int32)
    query_doc = lax.dynamic_slice_in_dim(doc_list, query_start, tok_rows)
    padded_docs = jnp.concatenate([jnp.full((reach_rows * tok_rows,), -1, jnp.int32), doc_list])
    key_doc = lax.dynamic_slice_in_dim(padded_docs, query_start, span_rows)
    key_shared = shared_lookup(key_doc, shared_flags)
    allowed = (
        (key_pos[None, :] >= 0)
        & (key_pos[None, :] <= query_pos[:, None])
        & (query_pos[:, None] - key_pos[None, :] < WINDOW)
    )
    allowed = allowed & ((key_doc[None, :] == query_doc[:, None]) | (key_shared[None, :] == 1))
    query_grad, key_sum, value_sum = attend(query_local, key_near, value_near, d_attn, allowed)
    query_handed = from_behind(query_grad, "pipe", -1)
    pair_sum = jnp.concatenate([key_sum, value_sum], axis=1)
    pair_sum = pair_sum.reshape(reach_rows + 1, tok_rows, 2 * key_width)
    even_part = pair_sum[0::2]
    odd_part = pair_sum[1::2]
    partner = lax.ppermute(
        odd_part, "row", [(i, i ^ 1) for i in range(lax.axis_size("row"))]
    )
    zero_block = jnp.zeros_like(odd_part[:1])
    partner_aligned = jnp.where(
        core_bit == 0,
        jnp.concatenate([zero_block, partner], axis=0),
        jnp.concatenate([partner, zero_block], axis=0),
    )
    chip_sum = even_part + partner_aligned
    running = chip_sum[0]
    for step in range(1, reach_rows // 2 + 1):
        running = from_behind(running, "row", -2) + chip_sum[step]
    key_total = running[:, :key_width]
    value_total = running[:, key_width:]
    key_handed, value_handed = from_behind(
        (key_total.astype(jnp.bfloat16), value_total.astype(jnp.bfloat16)), "pipe", -1
    )
    return (query_handed[None], key_handed[None], value_handed[None], grad_handed[None])


def solution(mesh):
    in_specs = (
        P("pipe", "row", "col"),
        P("pipe", "col", "row"),
        P("pipe", "row", "col"),
        P("pipe", "row", "col"),
        P("pipe", "row", "col"),
        P("pipe", None),
        P("pipe", None),
    )
    out_specs = (
        P("pipe", "row", "col"),
        P("pipe", "row", "col"),
        P("pipe", "row", "col"),
        P("pipe", "row", "col"),
    )
    return jax.shard_map(
        per_device, mesh=mesh, in_specs=in_specs, out_specs=out_specs, check_vma=False
    )
```

```python
import jax
import jax.numpy as jnp
from jax import lax
from jax.sharding import PartitionSpec as P

HD = 128
WINDOW = 4096


logit_cap = 50.0
score_scale = 144.0 ** (-0.5)


def from_behind(block, axis, distance):
    devices = range(lax.axis_size(axis))
    route = [(i - distance, i) for i in devices if i - distance in devices]
    return lax.ppermute(block, axis, route)


def cyclic_shift(block, axis, distance):
    size = lax.axis_size(axis)
    return lax.ppermute(block, axis, [(i, (i + distance) % size) for i in range(size)])


def ring_gather(block, axis):
    size = lax.axis_size(axis)
    ahead = [block]
    behind = []
    forward = block
    backward = block
    for _ in range(size // 2):
        forward = cyclic_shift(forward, axis, 1)
        behind.append(forward)
    for _ in range((size - 1) // 2):
        backward = cyclic_shift(backward, axis, -1)
        ahead.append(backward)
    relative = jnp.stack(ahead + behind[::-1], axis=0)
    rolled = jnp.roll(relative, lax.axis_index(axis), axis=0)
    return jnp.moveaxis(rolled, 0, 1).reshape(block.shape[0], size * block.shape[1])


def attend(query_act, key_near, value_near, d_attn, allowed):
    tok_rows = query_act.shape[0]
    span_rows = key_near.shape[0]
    key_width = key_near.shape[1]
    groups = key_width // HD
    query_g = query_act.reshape(tok_rows, groups, 2, HD)
    attn_g = d_attn.reshape(tok_rows, groups, 2, HD)
    key_g = key_near.reshape(span_rows, groups, HD)
    value_g = value_near.reshape(span_rows, groups, HD)
    raw_scores = (
        jnp.einsum("qgrd,kgd->grqk", query_g, key_g, preferred_element_type=jnp.float32)
        * score_scale
    )
    capped = jnp.tanh(raw_scores / logit_cap)
    weights = jnp.where(allowed[None, None], jnp.exp(logit_cap * capped), 0.0)
    attn_probs = weights / jnp.sum(weights, axis=-1, keepdims=True)
    probs_low = attn_probs.astype(jnp.bfloat16)
    value_sum = jnp.einsum(
        "grqk,qgrd->kgd", probs_low, attn_g, preferred_element_type=jnp.float32
    )
    grad_probs = jnp.einsum(
        "qgrd,kgd->grqk", attn_g, value_g, preferred_element_type=jnp.float32
    )
    row_delta = jnp.sum(attn_probs * grad_probs, axis=-1, keepdims=True)
    grad_raw = (
        attn_probs * (grad_probs - row_delta) * (1.0 - capped * capped) * score_scale
    ).astype(jnp.bfloat16)
    query_grad = jnp.einsum(
        "grqk,kgd->qgrd", grad_raw, key_g, preferred_element_type=jnp.float32
    ).astype(jnp.bfloat16)
    key_sum = jnp.einsum(
        "grqk,qgrd->kgd", grad_raw, query_g, preferred_element_type=jnp.float32
    )
    return (
        query_grad.reshape(tok_rows, key_width * 2),
        key_sum.reshape(span_rows, key_width),
        value_sum.reshape(span_rows, key_width),
    )


def shared_lookup(key_doc, shared_flags):
    doc_numbers = jnp.arange(shared_flags.shape[0], dtype=jnp.int32)
    return jnp.sum(
        jnp.where(key_doc[:, None] == doc_numbers[None, :], shared_flags[None, :], 0), axis=1
    )


def per_device(grad_out, out_weight, query_act, key_act, value_act, doc_ids, doc_shared):
    grad_tile = grad_out[0]
    tok_rows = grad_tile.shape[0]
    grad_handed = from_behind(grad_tile, "pipe", -1)
    grad_rows = ring_gather(grad_tile, "col")
    d_attn = lax.dot_general(
        grad_rows,
        lax.all_gather(out_weight[0], "row", axis=1, tiled=True),
        (((1,), (1,)), ((), ())),
        preferred_element_type=jnp.float32,
    ).astype(jnp.bfloat16)
    row_count = lax.axis_size("row")
    pipe_count = lax.axis_size("pipe")
    reach_rows = min(row_count - 1, WINDOW // tok_rows)
    hops = reach_rows // 2
    row_index = lax.axis_index("row")
    core_bit = row_index % 2
    partner_index = row_index + 1 - 2 * core_bit
    swap_pairs = [(i, i ^ 1) for i in range(row_count)]
    query_start = row_index * tok_rows
    doc_list = doc_ids[0]
    shared_flags = doc_shared[0]
    query_local = query_act[0]
    key_local = key_act[0]
    value_local = value_act[0]
    key_width = key_local.shape[1]
    pair_local = jnp.concatenate([key_local, value_local], axis=1)
    moving = pair_local
    same_blocks = [pair_local]
    for _ in range(hops):
        moving = from_behind(moving, "row", 2)
        same_blocks.append(moving)
    same_stack = jnp.stack(same_blocks, axis=0)
    other_stack = lax.ppermute(same_stack, "row", swap_pairs)
    pair_near = jnp.concatenate([same_stack, other_stack], axis=0).reshape(-1, 2 * key_width)
    back_steps = 2 * jnp.arange(hops + 1, dtype=jnp.int32)
    block_ids = jnp.concatenate([row_index - back_steps, partner_index - back_steps])
    key_pos = (block_ids[:, None] * tok_rows + jnp.arange(tok_rows, dtype=jnp.int32)[None, :]).reshape(-1)
    query_pos = query_start + jnp.arange(tok_rows, dtype=jnp.int32)
    query_doc = lax.dynamic_slice_in_dim(doc_list, query_start, tok_rows)
    lead = reach_rows * tok_rows
    padded_docs = jnp.concatenate([jnp.full((lead,), -1, jnp.int32), doc_list])
    key_doc = jnp.take(padded_docs, jnp.clip(key_pos + lead, 0, padded_docs.shape[0] - 1))
    key_shared = shared_lookup(key_doc, shared_flags)
    allowed = (
        (key_pos[None, :] >= 0)
        & (key_pos[None, :] <= query_pos[:, None])
        & (query_pos[:, None] - key_pos[None, :] < WINDOW)
    )
    allowed = allowed & ((key_doc[None, :] == query_doc[:, None]) | (key_shared[None, :] == 1))
    query_grad, key_sum, value_sum = attend(
        query_local, pair_near[:, :key_width], pair_near[:, key_width:], d_attn, allowed
    )
    query_handed = from_behind(query_grad, "pipe", -1)
    pair_sum = jnp.concatenate([key_sum, value_sum], axis=1).reshape(
        2, hops + 1, tok_rows, 2 * key_width
    )
    chip_sum = pair_sum[0] + lax.ppermute(pair_sum[1], "row", swap_pairs)
    own_handed = from_behind(chip_sum[0], "pipe", -1)
    running = chip_sum[hops]
    for step in range(1, hops):
        running = from_behind(running, "row", -2) + chip_sum[hops - step]
    last_pairs = [
        (p * row_count + r, (p - 1) * row_count + r - 2)
        for p in range(1, pipe_count)
        for r in range(2, row_count)
    ]
    total = lax.ppermute(running, ("pipe", "row"), last_pairs) + own_handed
    key_handed = total[:, :key_width].astype(jnp.bfloat16)
    value_handed = total[:, key_width:].astype(jnp.bfloat16)
    return (query_handed[None], key_handed[None], value_handed[None], grad_handed[None])


def solution(mesh):
    in_specs = (
        P("pipe", "row", "col"),
        P("pipe", "col", "row"),
        P("pipe", "row", "col"),
        P("pipe", "row", "col"),
        P("pipe", "row", "col"),
        P("pipe", None),
        P("pipe", None),
    )
    out_specs = (
        P("pipe", "row", "col"),
        P("pipe", "row", "col"),
        P("pipe", "row", "col"),
        P("pipe", "row", "col"),
    )
    return jax.shard_map(
        per_device, mesh=mesh, in_specs=in_specs, out_specs=out_specs, check_vma=False
    )
```

```python
import jax
import jax.numpy as jnp
from jax import lax
from jax.sharding import PartitionSpec as P

HD = 128
WINDOW = 4096


logit_cap = 50.0
score_scale = 144.0 ** (-0.5)


def from_behind(block, axis, distance):
    devices = range(lax.axis_size(axis))
    route = [(i - distance, i) for i in devices if i - distance in devices]
    return lax.ppermute(block, axis, route)


def cyclic_shift(block, axis, distance):
    size = lax.axis_size(axis)
    return lax.ppermute(block, axis, [(i, (i + distance) % size) for i in range(size)])


def ring_gather(block, axis):
    size = lax.axis_size(axis)
    ahead = [block]
    behind = []
    forward = block
    backward = block
    for _ in range(size // 2):
        forward = cyclic_shift(forward, axis, 1)
        behind.append(forward)
    for _ in range((size - 1) // 2):
        backward = cyclic_shift(backward, axis, -1)
        ahead.append(backward)
    relative = jnp.stack(ahead + behind[::-1], axis=0)
    rolled = jnp.roll(relative, lax.axis_index(axis), axis=0)
    return jnp.moveaxis(rolled, 0, 1).reshape(block.shape[0], size * block.shape[1])


def attend(query_act, key_near, value_near, d_attn, allowed):
    tok_rows = query_act.shape[0]
    span_rows = key_near.shape[0]
    key_width = key_near.shape[1]
    groups = key_width // HD
    query_g = query_act.reshape(tok_rows, groups, 2, HD)
    attn_g = d_attn.reshape(tok_rows, groups, 2, HD)
    key_g = key_near.reshape(span_rows, groups, HD)
    value_g = value_near.reshape(span_rows, groups, HD)
    raw_scores = (
        jnp.einsum("qgrd,kgd->grqk", query_g, key_g, preferred_element_type=jnp.float32)
        * score_scale
    )
    capped = jnp.tanh(raw_scores / logit_cap)
    weights = jnp.where(allowed[None, None], jnp.exp(logit_cap * capped), 0.0)
    attn_probs = weights / jnp.sum(weights, axis=-1, keepdims=True)
    probs_low = attn_probs.astype(jnp.bfloat16)
    value_sum = jnp.einsum(
        "grqk,qgrd->kgd", probs_low, attn_g, preferred_element_type=jnp.float32
    )
    grad_probs = jnp.einsum(
        "qgrd,kgd->grqk", attn_g, value_g, preferred_element_type=jnp.float32
    )
    row_delta = jnp.sum(attn_probs * grad_probs, axis=-1, keepdims=True)
    grad_raw = (
        attn_probs * (grad_probs - row_delta) * (1.0 - capped * capped) * score_scale
    ).astype(jnp.bfloat16)
    query_grad = jnp.einsum(
        "grqk,kgd->qgrd", grad_raw, key_g, preferred_element_type=jnp.float32
    ).astype(jnp.bfloat16)
    key_sum = jnp.einsum(
        "grqk,qgrd->kgd", grad_raw, query_g, preferred_element_type=jnp.float32
    )
    return (
        query_grad.reshape(tok_rows, key_width * 2),
        key_sum.reshape(span_rows, key_width),
        value_sum.reshape(span_rows, key_width),
    )


def shared_lookup(key_doc, shared_flags):
    doc_numbers = jnp.arange(shared_flags.shape[0], dtype=jnp.int32)
    return jnp.sum(
        jnp.where(key_doc[:, None] == doc_numbers[None, :], shared_flags[None, :], 0), axis=1
    )


def per_device(grad_out, out_weight, query_act, key_act, value_act, doc_ids, doc_shared):
    grad_tile = grad_out[0]
    tok_rows = grad_tile.shape[0]
    grad_handed = from_behind(grad_tile, "pipe", -1)
    grad_rows = ring_gather(grad_tile, "col")
    d_attn = lax.dot_general(
        grad_rows,
        lax.all_gather(out_weight[0], "row", axis=1, tiled=True),
        (((1,), (1,)), ((), ())),
        preferred_element_type=jnp.float32,
    ).astype(jnp.bfloat16)
    row_count = lax.axis_size("row")
    pipe_count = lax.axis_size("pipe")
    reach_rows = min(row_count - 1, WINDOW // tok_rows)
    hops = reach_rows // 2
    row_index = lax.axis_index("row")
    core_bit = row_index % 2
    partner_index = row_index + 1 - 2 * core_bit
    swap_pairs = [(i, i ^ 1) for i in range(row_count)]
    query_start = row_index * tok_rows
    doc_list = doc_ids[0]
    shared_flags = doc_shared[0]
    query_local = query_act[0]
    key_local = key_act[0]
    value_local = value_act[0]
    key_width = key_local.shape[1]
    pair_local = jnp.concatenate([key_local, value_local], axis=1)
    moving = pair_local
    same_blocks = [pair_local]
    for _ in range(hops):
        moving = from_behind(moving, "row", 2)
        same_blocks.append(moving)
    same_stack = jnp.stack(same_blocks, axis=0)
    other_stack = lax.ppermute(same_stack, "row", swap_pairs)
    pair_near = jnp.concatenate([same_stack, other_stack], axis=0).reshape(-1, 2 * key_width)
    back_steps = 2 * jnp.arange(hops + 1, dtype=jnp.int32)
    block_ids = jnp.concatenate([row_index - back_steps, partner_index - back_steps])
    key_pos = (block_ids[:, None] * tok_rows + jnp.arange(tok_rows, dtype=jnp.int32)[None, :]).reshape(-1)
    query_pos = query_start + jnp.arange(tok_rows, dtype=jnp.int32)
    query_doc = lax.dynamic_slice_in_dim(doc_list, query_start, tok_rows)
    lead = reach_rows * tok_rows
    padded_docs = jnp.concatenate([jnp.full((lead,), -1, jnp.int32), doc_list])
    run_rows = (2 * hops + 1) * tok_rows
    key_doc = jnp.concatenate(
        [
            lax.dynamic_slice_in_dim(padded_docs, start * tok_rows, run_rows)
            .reshape(2 * hops + 1, tok_rows)[::-2]
            .reshape(-1)
            for start in (row_index, partner_index)
        ]
    )
    key_shared = shared_lookup(key_doc, shared_flags)
    allowed = (
        (key_pos[None, :] >= 0)
        & (key_pos[None, :] <= query_pos[:, None])
        & (query_pos[:, None] - key_pos[None, :] < WINDOW)
    )
    allowed = allowed & ((key_doc[None, :] == query_doc[:, None]) | (key_shared[None, :] == 1))
    query_grad, key_sum, value_sum = attend(
        query_local, pair_near[:, :key_width], pair_near[:, key_width:], d_attn, allowed
    )
    query_handed = from_behind(query_grad, "pipe", -1)
    pair_sum = jnp.concatenate([key_sum, value_sum], axis=1).reshape(
        2, hops + 1, tok_rows, 2 * key_width
    )
    chip_sum = pair_sum[0] + lax.ppermute(pair_sum[1], "row", swap_pairs)
    own_handed = from_behind(chip_sum[0], "pipe", -1)
    running = chip_sum[hops]
    for step in range(1, hops):
        running = from_behind(running, "row", -2) + chip_sum[hops - step]
    last_pairs = [
        (p * row_count + r, (p - 1) * row_count + r - 2)
        for p in range(1, pipe_count)
        for r in range(2, row_count)
    ]
    total = lax.ppermute(running, ("pipe", "row"), last_pairs) + own_handed
    key_handed = total[:, :key_width].astype(jnp.bfloat16)
    value_handed = total[:, key_width:].astype(jnp.bfloat16)
    return (query_handed[None], key_handed[None], value_handed[None], grad_handed[None])


def solution(mesh):
    in_specs = (
        P("pipe", "row", "col"),
        P("pipe", "col", "row"),
        P("pipe", "row", "col"),
        P("pipe", "row", "col"),
        P("pipe", "row", "col"),
        P("pipe", None),
        P("pipe", None),
    )
    out_specs = (
        P("pipe", "row", "col"),
        P("pipe", "row", "col"),
        P("pipe", "row", "col"),
        P("pipe", "row", "col"),
    )
    return jax.shard_map(
        per_device, mesh=mesh, in_specs=in_specs, out_specs=out_specs, check_vma=False
    )
```

```python
import jax
import jax.numpy as jnp
from jax import lax
from jax.sharding import PartitionSpec as P

HD = 128
WINDOW = 4096


logit_cap = 50.0
score_scale = 144.0 ** (-0.5)


def from_behind(block, axis, distance):
    devices = range(lax.axis_size(axis))
    route = [(i - distance, i) for i in devices if i - distance in devices]
    return lax.ppermute(block, axis, route)


def cyclic_shift(block, axis, distance):
    size = lax.axis_size(axis)
    return lax.ppermute(block, axis, [(i, (i + distance) % size) for i in range(size)])


def ring_gather(block, axis):
    size = lax.axis_size(axis)
    ahead = [block]
    behind = []
    forward = block
    backward = block
    for _ in range(size // 2):
        forward = cyclic_shift(forward, axis, 1)
        behind.append(forward)
    for _ in range((size - 1) // 2):
        backward = cyclic_shift(backward, axis, -1)
        ahead.append(backward)
    relative = jnp.stack(ahead + behind[::-1], axis=0)
    rolled = jnp.roll(relative, lax.axis_index(axis), axis=0)
    return jnp.moveaxis(rolled, 0, 1).reshape(block.shape[0], size * block.shape[1])


def attend(query_act, key_near, value_near, d_attn, allowed):
    tok_rows = query_act.shape[0]
    span_rows = key_near.shape[0]
    key_width = key_near.shape[1]
    groups = key_width // HD
    query_g = query_act.reshape(tok_rows, groups, 2, HD)
    attn_g = d_attn.reshape(tok_rows, groups, 2, HD)
    key_g = key_near.reshape(span_rows, groups, HD)
    value_g = value_near.reshape(span_rows, groups, HD)
    raw_scores = (
        jnp.einsum("qgrd,kgd->grqk", query_g, key_g, preferred_element_type=jnp.float32)
        * score_scale
    )
    capped = jnp.tanh(raw_scores / logit_cap)
    weights = jnp.where(allowed[None, None], jnp.exp(logit_cap * capped), 0.0)
    attn_probs = weights / jnp.sum(weights, axis=-1, keepdims=True)
    probs_low = attn_probs.astype(jnp.bfloat16)
    value_sum = jnp.einsum(
        "grqk,qgrd->kgd", probs_low, attn_g, preferred_element_type=jnp.float32
    )
    grad_probs = jnp.einsum(
        "qgrd,kgd->grqk", attn_g, value_g, preferred_element_type=jnp.float32
    )
    row_delta = jnp.sum(attn_probs * grad_probs, axis=-1, keepdims=True)
    grad_raw = (
        attn_probs * (grad_probs - row_delta) * (1.0 - capped * capped) * score_scale
    ).astype(jnp.bfloat16)
    query_grad = jnp.einsum(
        "grqk,kgd->qgrd", grad_raw, key_g, preferred_element_type=jnp.float32
    ).astype(jnp.bfloat16)
    key_sum = jnp.einsum(
        "grqk,qgrd->kgd", grad_raw, query_g, preferred_element_type=jnp.float32
    )
    return (
        query_grad.reshape(tok_rows, key_width * 2),
        key_sum.reshape(span_rows, key_width),
        value_sum.reshape(span_rows, key_width),
    )


def shared_lookup(key_doc, shared_flags):
    doc_numbers = jnp.arange(shared_flags.shape[0], dtype=jnp.int32)
    return jnp.sum(
        jnp.where(key_doc[:, None] == doc_numbers[None, :], shared_flags[None, :], 0), axis=1
    )


def per_device(grad_out, out_weight, query_act, key_act, value_act, doc_ids, doc_shared):
    grad_tile = grad_out[0]
    tok_rows = grad_tile.shape[0]
    grad_handed = from_behind(grad_tile, "pipe", -1)
    grad_rows = ring_gather(grad_tile, "col")
    d_attn = lax.dot_general(
        grad_rows,
        lax.all_gather(out_weight[0], "row", axis=1, tiled=True),
        (((1,), (1,)), ((), ())),
        preferred_element_type=jnp.float32,
    ).astype(jnp.bfloat16)
    row_count = lax.axis_size("row")
    pipe_count = lax.axis_size("pipe")
    reach_rows = min(row_count - 1, WINDOW // tok_rows)
    hops = reach_rows // 2
    row_index = lax.axis_index("row")
    core_bit = row_index % 2
    partner_index = row_index + 1 - 2 * core_bit
    swap_pairs = [(i, i ^ 1) for i in range(row_count)]
    query_start = row_index * tok_rows
    doc_list = doc_ids[0]
    shared_flags = doc_shared[0]
    query_local = query_act[0]
    key_local = key_act[0]
    value_local = value_act[0]
    key_width = key_local.shape[1]
    pair_local = jnp.concatenate([key_local, value_local], axis=1)
    moving = pair_local
    same_blocks = [pair_local]
    for _ in range(hops):
        moving = from_behind(moving, "row", 2)
        same_blocks.append(moving)
    same_stack = jnp.stack(same_blocks, axis=0)
    other_stack = lax.ppermute(same_stack, "row", swap_pairs)
    pair_near = jnp.concatenate([same_stack, other_stack], axis=0).reshape(-1, 2 * key_width)
    back_steps = 2 * jnp.arange(hops + 1, dtype=jnp.int32)
    block_ids = jnp.concatenate([row_index - back_steps, partner_index - back_steps])
    key_pos = (block_ids[:, None] * tok_rows + jnp.arange(tok_rows, dtype=jnp.int32)[None, :]).reshape(-1)
    query_pos = query_start + jnp.arange(tok_rows, dtype=jnp.int32)
    query_doc = lax.dynamic_slice_in_dim(doc_list, query_start, tok_rows)
    lead = reach_rows * tok_rows
    padded_docs = jnp.concatenate([jnp.full((lead,), -1, jnp.int32), doc_list])
    run_rows = (2 * hops + 1) * tok_rows
    key_doc = jnp.concatenate(
        [
            lax.dynamic_slice_in_dim(padded_docs, start * tok_rows, run_rows)
            .reshape(2 * hops + 1, tok_rows)[::-2]
            .reshape(-1)
            for start in (row_index, partner_index)
        ]
    )
    key_shared = shared_lookup(key_doc, shared_flags)
    allowed = (
        (key_pos[None, :] >= 0)
        & (key_pos[None, :] <= query_pos[:, None])
        & (query_pos[:, None] - key_pos[None, :] < WINDOW)
    )
    allowed = allowed & ((key_doc[None, :] == query_doc[:, None]) | (key_shared[None, :] == 1))
    query_grad, key_sum, value_sum = attend(
        query_local, pair_near[:, :key_width], pair_near[:, key_width:], d_attn, allowed
    )
    query_grad, key_sum, value_sum = lax.optimization_barrier((query_grad, key_sum, value_sum))
    query_handed = from_behind(query_grad, "pipe", -1)
    pair_sum = jnp.concatenate([key_sum, value_sum], axis=1).reshape(
        2, hops + 1, tok_rows, 2 * key_width
    )
    chip_sum = pair_sum[0] + lax.ppermute(pair_sum[1], "row", swap_pairs)
    own_handed = from_behind(chip_sum[0], "pipe", -1)
    running = chip_sum[hops]
    for step in range(1, hops):
        running = from_behind(running, "row", -2) + chip_sum[hops - step]
        if step == hops // 2:
            running, query_handed = lax.optimization_barrier((running, query_handed))
    last_pairs = [
        (p * row_count + r, (p - 1) * row_count + r - 2)
        for p in range(1, pipe_count)
        for r in range(2, row_count)
    ]
    total = lax.ppermute(running, ("pipe", "row"), last_pairs) + own_handed
    key_handed = total[:, :key_width].astype(jnp.bfloat16)
    value_handed = total[:, key_width:].astype(jnp.bfloat16)
    return (query_handed[None], key_handed[None], value_handed[None], grad_handed[None])


def solution(mesh):
    in_specs = (
        P("pipe", "row", "col"),
        P("pipe", "col", "row"),
        P("pipe", "row", "col"),
        P("pipe", "row", "col"),
        P("pipe", "row", "col"),
        P("pipe", None),
        P("pipe", None),
    )
    out_specs = (
        P("pipe", "row", "col"),
        P("pipe", "row", "col"),
        P("pipe", "row", "col"),
        P("pipe", "row", "col"),
    )
    return jax.shard_map(
        per_device, mesh=mesh, in_specs=in_specs, out_specs=out_specs, check_vma=False
    )
```

```python
import jax
import jax.numpy as jnp
from jax import lax
from jax.sharding import PartitionSpec as P

HD = 128
WINDOW = 4096


logit_cap = 50.0
score_scale = 144.0 ** (-0.5)


def from_behind(block, axis, distance):
    devices = range(lax.axis_size(axis))
    route = [(i - distance, i) for i in devices if i - distance in devices]
    return lax.ppermute(block, axis, route)


def cyclic_shift(block, axis, distance):
    size = lax.axis_size(axis)
    return lax.ppermute(block, axis, [(i, (i + distance) % size) for i in range(size)])


def ring_gather(block, axis):
    size = lax.axis_size(axis)
    ahead = [block]
    behind = []
    forward = block
    backward = block
    for _ in range(size // 2):
        forward = cyclic_shift(forward, axis, 1)
        behind.append(forward)
    for _ in range((size - 1) // 2):
        backward = cyclic_shift(backward, axis, -1)
        ahead.append(backward)
    relative = jnp.stack(ahead + behind[::-1], axis=0)
    rolled = jnp.roll(relative, lax.axis_index(axis), axis=0)
    return jnp.moveaxis(rolled, 0, 1).reshape(block.shape[0], size * block.shape[1])


def attend(query_act, key_near, value_near, d_attn, allowed):
    tok_rows = query_act.shape[0]
    span_rows = key_near.shape[0]
    key_width = key_near.shape[1]
    groups = key_width // HD
    query_g = query_act.reshape(tok_rows, groups, 2, HD)
    attn_g = d_attn.reshape(tok_rows, groups, 2, HD)
    key_g = key_near.reshape(span_rows, groups, HD)
    value_g = value_near.reshape(span_rows, groups, HD)
    raw_scores = (
        jnp.einsum("qgrd,kgd->grqk", query_g, key_g, preferred_element_type=jnp.float32)
        * score_scale
    )
    capped = jnp.tanh(raw_scores / logit_cap)
    weights = jnp.where(allowed[None, None], jnp.exp(logit_cap * capped), 0.0)
    attn_probs = weights / jnp.sum(weights, axis=-1, keepdims=True)
    probs_low = attn_probs.astype(jnp.bfloat16)
    value_sum = jnp.einsum(
        "grqk,qgrd->kgd", probs_low, attn_g, preferred_element_type=jnp.float32
    )
    grad_probs = jnp.einsum(
        "qgrd,kgd->grqk", attn_g, value_g, preferred_element_type=jnp.float32
    )
    row_delta = jnp.sum(attn_probs * grad_probs, axis=-1, keepdims=True)
    grad_raw = (
        attn_probs * (grad_probs - row_delta) * (1.0 - capped * capped) * score_scale
    ).astype(jnp.bfloat16)
    query_grad = jnp.einsum(
        "grqk,kgd->qgrd", grad_raw, key_g, preferred_element_type=jnp.float32
    ).astype(jnp.bfloat16)
    key_sum = jnp.einsum(
        "grqk,qgrd->kgd", grad_raw, query_g, preferred_element_type=jnp.float32
    )
    return (
        query_grad.reshape(tok_rows, key_width * 2),
        key_sum.reshape(span_rows, key_width),
        value_sum.reshape(span_rows, key_width),
    )


def shared_lookup(key_doc, shared_flags):
    doc_numbers = jnp.arange(shared_flags.shape[0], dtype=jnp.int32)
    return jnp.sum(
        jnp.where(key_doc[:, None] == doc_numbers[None, :], shared_flags[None, :], 0), axis=1
    )


def per_device(grad_out, out_weight, query_act, key_act, value_act, doc_ids, doc_shared):
    grad_tile = grad_out[0]
    tok_rows = grad_tile.shape[0]
    grad_handed = from_behind(grad_tile, "pipe", -1)
    grad_rows = ring_gather(grad_tile, "col")
    d_attn = lax.dot_general(
        grad_rows,
        lax.all_gather(out_weight[0], "row", axis=1, tiled=True),
        (((1,), (1,)), ((), ())),
        preferred_element_type=jnp.float32,
    ).astype(jnp.bfloat16)
    row_count = lax.axis_size("row")
    pipe_count = lax.axis_size("pipe")
    reach_rows = min(row_count - 1, WINDOW // tok_rows)
    hops = reach_rows // 2
    row_index = lax.axis_index("row")
    core_bit = row_index % 2
    partner_index = row_index + 1 - 2 * core_bit
    swap_pairs = [(i, i ^ 1) for i in range(row_count)]
    query_start = row_index * tok_rows
    doc_list = doc_ids[0]
    shared_flags = doc_shared[0]
    query_local = query_act[0]
    key_local = key_act[0]
    value_local = value_act[0]
    key_width = key_local.shape[1]
    pair_local = jnp.concatenate([key_local, value_local], axis=1)
    moving = pair_local
    same_blocks = [pair_local]
    for _ in range(hops):
        moving = from_behind(moving, "row", 2)
        same_blocks.append(moving)
    same_stack = jnp.stack(same_blocks, axis=0)
    other_stack = lax.ppermute(same_stack, "row", swap_pairs)
    pair_near = jnp.concatenate([same_stack, other_stack], axis=0).reshape(-1, 2 * key_width)
    back_steps = 2 * jnp.arange(hops + 1, dtype=jnp.int32)
    block_ids = jnp.concatenate([row_index - back_steps, partner_index - back_steps])
    key_pos = (block_ids[:, None] * tok_rows + jnp.arange(tok_rows, dtype=jnp.int32)[None, :]).reshape(-1)
    query_pos = query_start + jnp.arange(tok_rows, dtype=jnp.int32)
    query_doc = lax.dynamic_slice_in_dim(doc_list, query_start, tok_rows)
    lead = reach_rows * tok_rows
    padded_docs = jnp.concatenate([jnp.full((lead,), -1, jnp.int32), doc_list])
    run_rows = (2 * hops + 1) * tok_rows
    key_doc = jnp.concatenate(
        [
            lax.dynamic_slice_in_dim(padded_docs, start * tok_rows, run_rows)
            .reshape(2 * hops + 1, tok_rows)[::-2]
            .reshape(-1)
            for start in (row_index, partner_index)
        ]
    )
    key_shared = shared_lookup(key_doc, shared_flags)
    allowed = (
        (key_pos[None, :] >= 0)
        & (key_pos[None, :] <= query_pos[:, None])
        & (query_pos[:, None] - key_pos[None, :] < WINDOW)
    )
    allowed = allowed & ((key_doc[None, :] == query_doc[:, None]) | (key_shared[None, :] == 1))
    query_grad, key_sum, value_sum = attend(
        query_local, pair_near[:, :key_width], pair_near[:, key_width:], d_attn, allowed
    )
    query_grad, key_sum, value_sum = lax.optimization_barrier((query_grad, key_sum, value_sum))
    query_handed = from_behind(query_grad, "pipe", -1)
    pair_sum = jnp.concatenate([key_sum, value_sum], axis=1).reshape(
        2, hops + 1, tok_rows, 2 * key_width
    )
    chip_sum = pair_sum[0] + lax.ppermute(pair_sum[1], "row", swap_pairs)
    own_handed = from_behind(chip_sum[0], "pipe", -1)
    running = chip_sum[hops]
    for step in range(1, hops):
        running = from_behind(running, "row", -2) + chip_sum[hops - step]
        if step == hops // 2:
            running, query_handed, own_handed = lax.optimization_barrier(
                (running, query_handed, own_handed)
            )
    last_pairs = [
        (p * row_count + r, (p - 1) * row_count + r - 2)
        for p in range(1, pipe_count)
        for r in range(2, row_count)
    ]
    total = lax.ppermute(running, ("pipe", "row"), last_pairs) + own_handed
    key_handed = total[:, :key_width].astype(jnp.bfloat16)
    value_handed = total[:, key_width:].astype(jnp.bfloat16)
    return (query_handed[None], key_handed[None], value_handed[None], grad_handed[None])


def solution(mesh):
    in_specs = (
        P("pipe", "row", "col"),
        P("pipe", "col", "row"),
        P("pipe", "row", "col"),
        P("pipe", "row", "col"),
        P("pipe", "row", "col"),
        P("pipe", None),
        P("pipe", None),
    )
    out_specs = (
        P("pipe", "row", "col"),
        P("pipe", "row", "col"),
        P("pipe", "row", "col"),
        P("pipe", "row", "col"),
    )
    return jax.shard_map(
        per_device, mesh=mesh, in_specs=in_specs, out_specs=out_specs, check_vma=False
    )
```

```python
import jax
import jax.numpy as jnp
from jax import lax
from jax.sharding import PartitionSpec as P

HD = 128
WINDOW = 4096


logit_cap = 50.0
score_scale = 144.0 ** (-0.5)


def from_behind(block, axis, distance):
    devices = range(lax.axis_size(axis))
    route = [(i - distance, i) for i in devices if i - distance in devices]
    return lax.ppermute(block, axis, route)


def cyclic_shift(block, axis, distance):
    size = lax.axis_size(axis)
    return lax.ppermute(block, axis, [(i, (i + distance) % size) for i in range(size)])


def ring_gather(block, axis):
    size = lax.axis_size(axis)
    ahead = [block]
    behind = []
    forward = block
    backward = block
    for _ in range(size // 2):
        forward = cyclic_shift(forward, axis, 1)
        behind.append(forward)
    for _ in range((size - 1) // 2):
        backward = cyclic_shift(backward, axis, -1)
        ahead.append(backward)
    relative = jnp.stack(ahead + behind[::-1], axis=0)
    rolled = jnp.roll(relative, lax.axis_index(axis), axis=0)
    return jnp.moveaxis(rolled, 0, 1).reshape(block.shape[0], size * block.shape[1])


def attend(query_act, key_near, value_near, d_attn, allowed):
    tok_rows = query_act.shape[0]
    span_rows = key_near.shape[0]
    key_width = key_near.shape[1]
    groups = key_width // HD
    query_g = query_act.reshape(tok_rows, groups, 2, HD)
    attn_g = d_attn.reshape(tok_rows, groups, 2, HD)
    key_g = key_near.reshape(span_rows, groups, HD)
    value_g = value_near.reshape(span_rows, groups, HD)
    raw_scores = (
        jnp.einsum("qgrd,kgd->grqk", query_g, key_g, preferred_element_type=jnp.float32)
        * score_scale
    )
    capped = jnp.tanh(raw_scores / logit_cap)
    weights = jnp.where(allowed[None, None], jnp.exp(logit_cap * capped), 0.0)
    attn_probs = weights / jnp.sum(weights, axis=-1, keepdims=True)
    probs_low = attn_probs.astype(jnp.bfloat16)
    value_sum = jnp.einsum(
        "grqk,qgrd->kgd", probs_low, attn_g, preferred_element_type=jnp.float32
    )
    grad_probs = jnp.einsum(
        "qgrd,kgd->grqk", attn_g, value_g, preferred_element_type=jnp.float32
    )
    row_delta = jnp.sum(attn_probs * grad_probs, axis=-1, keepdims=True)
    grad_raw = (
        attn_probs * (grad_probs - row_delta) * (1.0 - capped * capped) * score_scale
    ).astype(jnp.bfloat16)
    query_grad = jnp.einsum(
        "grqk,kgd->qgrd", grad_raw, key_g, preferred_element_type=jnp.float32
    ).astype(jnp.bfloat16)
    key_sum = jnp.einsum(
        "grqk,qgrd->kgd", grad_raw, query_g, preferred_element_type=jnp.float32
    )
    return (
        query_grad.reshape(tok_rows, key_width * 2),
        key_sum.reshape(span_rows, key_width),
        value_sum.reshape(span_rows, key_width),
    )


def shared_lookup(key_doc, shared_flags):
    doc_numbers = jnp.arange(shared_flags.shape[0], dtype=jnp.int32)
    return jnp.sum(
        jnp.where(key_doc[:, None] == doc_numbers[None, :], shared_flags[None, :], 0), axis=1
    )


def per_device(grad_out, out_weight, query_act, key_act, value_act, doc_ids, doc_shared):
    grad_tile = grad_out[0]
    tok_rows = grad_tile.shape[0]
    grad_handed = from_behind(grad_tile, "pipe", -1)
    grad_rows = ring_gather(grad_tile, "col")
    d_attn = lax.dot_general(
        grad_rows,
        lax.all_gather(out_weight[0], "row", axis=1, tiled=True),
        (((1,), (1,)), ((), ())),
        preferred_element_type=jnp.float32,
    ).astype(jnp.bfloat16)
    row_count = lax.axis_size("row")
    pipe_count = lax.axis_size("pipe")
    reach_rows = min(row_count - 1, WINDOW // tok_rows)
    hops = reach_rows // 2
    row_index = lax.axis_index("row")
    core_bit = row_index % 2
    partner_index = row_index + 1 - 2 * core_bit
    swap_pairs = [(i, i ^ 1) for i in range(row_count)]
    query_start = row_index * tok_rows
    doc_list = doc_ids[0]
    shared_flags = doc_shared[0]
    query_local = query_act[0]
    key_local = key_act[0]
    value_local = value_act[0]
    key_width = key_local.shape[1]
    pair_local = jnp.concatenate([key_local, value_local], axis=1)
    moving = pair_local
    same_blocks = [pair_local]
    for _ in range(hops):
        moving = from_behind(moving, "row", 2)
        same_blocks.append(moving)
    same_stack = jnp.stack(same_blocks, axis=0)
    other_stack = lax.ppermute(same_stack, "row", swap_pairs)
    pair_near = jnp.concatenate([same_stack, other_stack], axis=0).reshape(-1, 2 * key_width)
    back_steps = 2 * jnp.arange(hops + 1, dtype=jnp.int32)
    block_ids = jnp.concatenate([row_index - back_steps, partner_index - back_steps])
    key_pos = (block_ids[:, None] * tok_rows + jnp.arange(tok_rows, dtype=jnp.int32)[None, :]).reshape(-1)
    query_pos = query_start + jnp.arange(tok_rows, dtype=jnp.int32)
    query_doc = lax.dynamic_slice_in_dim(doc_list, query_start, tok_rows)
    lead = reach_rows * tok_rows
    padded_docs = jnp.concatenate([jnp.full((lead,), -1, jnp.int32), doc_list])
    run_rows = (2 * hops + 1) * tok_rows
    key_doc = jnp.concatenate(
        [
            lax.dynamic_slice_in_dim(padded_docs, start * tok_rows, run_rows)
            .reshape(2 * hops + 1, tok_rows)[::-2]
            .reshape(-1)
            for start in (row_index, partner_index)
        ]
    )
    key_shared = shared_lookup(key_doc, shared_flags)
    allowed = (
        (key_pos[None, :] >= 0)
        & (key_pos[None, :] <= query_pos[:, None])
        & (query_pos[:, None] - key_pos[None, :] < WINDOW)
    )
    allowed = allowed & ((key_doc[None, :] == query_doc[:, None]) | (key_shared[None, :] == 1))
    query_grad, key_sum, value_sum = attend(
        query_local, pair_near[:, :key_width], pair_near[:, key_width:], d_attn, allowed
    )
    query_grad, key_sum, value_sum = lax.optimization_barrier((query_grad, key_sum, value_sum))
    query_handed = from_behind(query_grad, "pipe", -1)
    pair_sum = jnp.concatenate([key_sum, value_sum], axis=1).reshape(
        2, hops + 1, tok_rows, 2 * key_width
    )
    far_sum = pair_sum[0][hops] + lax.ppermute(pair_sum[1][hops], "row", swap_pairs)
    chip_sum = pair_sum[0][:hops] + lax.ppermute(pair_sum[1][:hops], "row", swap_pairs)
    own_handed = from_behind(chip_sum[0], "pipe", -1)
    running = far_sum
    for step in range(1, hops):
        running = from_behind(running, "row", -2) + chip_sum[hops - step]
        if step == hops // 2:
            running, query_handed = lax.optimization_barrier((running, query_handed))
    last_pairs = [
        (p * row_count + r, (p - 1) * row_count + r - 2)
        for p in range(1, pipe_count)
        for r in range(2, row_count)
    ]
    total = lax.ppermute(running, ("pipe", "row"), last_pairs) + own_handed
    key_handed = total[:, :key_width].astype(jnp.bfloat16)
    value_handed = total[:, key_width:].astype(jnp.bfloat16)
    return (query_handed[None], key_handed[None], value_handed[None], grad_handed[None])


def solution(mesh):
    in_specs = (
        P("pipe", "row", "col"),
        P("pipe", "col", "row"),
        P("pipe", "row", "col"),
        P("pipe", "row", "col"),
        P("pipe", "row", "col"),
        P("pipe", None),
        P("pipe", None),
    )
    out_specs = (
        P("pipe", "row", "col"),
        P("pipe", "row", "col"),
        P("pipe", "row", "col"),
        P("pipe", "row", "col"),
    )
    return jax.shard_map(
        per_device, mesh=mesh, in_specs=in_specs, out_specs=out_specs, check_vma=False
    )
```

```python
import jax
import jax.numpy as jnp
from jax import lax
from jax.sharding import PartitionSpec as P

HD = 128
WINDOW = 4096


logit_cap = 50.0
score_scale = 144.0 ** (-0.5)


def from_behind(block, axis, distance):
    devices = range(lax.axis_size(axis))
    route = [(i - distance, i) for i in devices if i - distance in devices]
    return lax.ppermute(block, axis, route)


def cyclic_shift(block, axis, distance):
    size = lax.axis_size(axis)
    return lax.ppermute(block, axis, [(i, (i + distance) % size) for i in range(size)])


def ring_gather(block, axis):
    size = lax.axis_size(axis)
    ahead = [block]
    behind = []
    forward = block
    backward = block
    for _ in range(size // 2):
        forward = cyclic_shift(forward, axis, 1)
        behind.append(forward)
    for _ in range((size - 1) // 2):
        backward = cyclic_shift(backward, axis, -1)
        ahead.append(backward)
    relative = jnp.stack(ahead + behind[::-1], axis=0)
    rolled = jnp.roll(relative, lax.axis_index(axis), axis=0)
    return jnp.moveaxis(rolled, 0, 1).reshape(block.shape[0], size * block.shape[1])


def attend(query_act, key_near, value_near, d_attn, allowed):
    tok_rows = query_act.shape[0]
    span_rows = key_near.shape[0]
    key_width = key_near.shape[1]
    groups = key_width // HD
    query_g = query_act.reshape(tok_rows, groups, 2, HD)
    attn_g = d_attn.reshape(tok_rows, groups, 2, HD)
    key_g = key_near.reshape(span_rows, groups, HD)
    value_g = value_near.reshape(span_rows, groups, HD)
    raw_scores = (
        jnp.einsum("qgrd,kgd->grqk", query_g, key_g, preferred_element_type=jnp.float32)
        * score_scale
    )
    capped = jnp.tanh(raw_scores / logit_cap)
    weights = jnp.where(allowed[None, None], jnp.exp(logit_cap * capped), 0.0)
    attn_probs = weights / jnp.sum(weights, axis=-1, keepdims=True)
    probs_low = attn_probs.astype(jnp.bfloat16)
    value_sum = jnp.einsum(
        "grqk,qgrd->kgd", probs_low, attn_g, preferred_element_type=jnp.float32
    )
    grad_probs = jnp.einsum(
        "qgrd,kgd->grqk", attn_g, value_g, preferred_element_type=jnp.float32
    )
    row_delta = jnp.sum(attn_probs * grad_probs, axis=-1, keepdims=True)
    grad_raw = (
        attn_probs * (grad_probs - row_delta) * (1.0 - capped * capped) * score_scale
    ).astype(jnp.bfloat16)
    query_grad = jnp.einsum(
        "grqk,kgd->qgrd", grad_raw, key_g, preferred_element_type=jnp.float32
    ).astype(jnp.bfloat16)
    key_sum = jnp.einsum(
        "grqk,qgrd->kgd", grad_raw, query_g, preferred_element_type=jnp.float32
    )
    return (
        query_grad.reshape(tok_rows, key_width * 2),
        key_sum.reshape(span_rows, key_width),
        value_sum.reshape(span_rows, key_width),
    )


def shared_lookup(key_doc, shared_flags):
    doc_numbers = jnp.arange(shared_flags.shape[0], dtype=jnp.int32)
    return jnp.sum(
        jnp.where(key_doc[:, None] == doc_numbers[None, :], shared_flags[None, :], 0), axis=1
    )


def per_device(grad_out, out_weight, query_act, key_act, value_act, doc_ids, doc_shared):
    grad_tile = grad_out[0]
    tok_rows = grad_tile.shape[0]
    grad_handed = from_behind(grad_tile, "pipe", -1)
    grad_rows = ring_gather(grad_tile, "col")
    d_attn = lax.dot_general(
        grad_rows,
        lax.all_gather(out_weight[0], "row", axis=1, tiled=True),
        (((1,), (1,)), ((), ())),
        preferred_element_type=jnp.float32,
    ).astype(jnp.bfloat16)
    row_count = lax.axis_size("row")
    pipe_count = lax.axis_size("pipe")
    reach_rows = min(row_count - 1, WINDOW // tok_rows)
    hops = reach_rows // 2
    row_index = lax.axis_index("row")
    core_bit = row_index % 2
    partner_index = row_index + 1 - 2 * core_bit
    swap_pairs = [(i, i ^ 1) for i in range(row_count)]
    query_start = row_index * tok_rows
    doc_list = doc_ids[0]
    shared_flags = doc_shared[0]
    query_local = query_act[0]
    key_local = key_act[0]
    value_local = value_act[0]
    key_width = key_local.shape[1]
    pair_local = jnp.concatenate([key_local, value_local], axis=1)
    moving = pair_local
    same_blocks = [pair_local]
    for _ in range(hops):
        moving = from_behind(moving, "row", 2)
        same_blocks.append(moving)
    same_stack = jnp.stack(same_blocks, axis=0)
    other_stack = lax.ppermute(same_stack, "row", swap_pairs)
    pair_near = jnp.concatenate([same_stack, other_stack], axis=0).reshape(-1, 2 * key_width)
    back_steps = 2 * jnp.arange(hops + 1, dtype=jnp.int32)
    block_ids = jnp.concatenate([row_index - back_steps, partner_index - back_steps])
    key_pos = (block_ids[:, None] * tok_rows + jnp.arange(tok_rows, dtype=jnp.int32)[None, :]).reshape(-1)
    query_pos = query_start + jnp.arange(tok_rows, dtype=jnp.int32)
    query_doc = lax.dynamic_slice_in_dim(doc_list, query_start, tok_rows)
    lead = reach_rows * tok_rows
    padded_docs = jnp.concatenate([jnp.full((lead,), -1, jnp.int32), doc_list])
    run_rows = (2 * hops + 1) * tok_rows
    key_doc = jnp.concatenate(
        [
            lax.dynamic_slice_in_dim(padded_docs, start * tok_rows, run_rows)
            .reshape(2 * hops + 1, tok_rows)[::-2]
            .reshape(-1)
            for start in (row_index, partner_index)
        ]
    )
    key_shared = shared_lookup(key_doc, shared_flags)
    allowed = (
        (key_pos[None, :] >= 0)
        & (key_pos[None, :] <= query_pos[:, None])
        & (query_pos[:, None] - key_pos[None, :] < WINDOW)
    )
    allowed = allowed & ((key_doc[None, :] == query_doc[:, None]) | (key_shared[None, :] == 1))
    query_grad, key_sum, value_sum = attend(
        query_local, pair_near[:, :key_width], pair_near[:, key_width:], d_attn, allowed
    )
    query_grad, key_sum, value_sum = lax.optimization_barrier((query_grad, key_sum, value_sum))
    query_handed = from_behind(query_grad, "pipe", -1)
    pair_sum = jnp.concatenate([key_sum, value_sum], axis=1).reshape(
        2, hops + 1, tok_rows, 2 * key_width
    )
    far_sum = pair_sum[0][hops] + lax.ppermute(pair_sum[1][hops], "row", swap_pairs)
    chip_sum = pair_sum[0][:hops] + lax.ppermute(pair_sum[1][:hops], "row", swap_pairs)
    own_handed = from_behind(chip_sum[0], "pipe", -1)
    running = far_sum
    for step in range(1, hops):
        running = from_behind(running, "row", -2) + chip_sum[hops - step]
        if step == hops // 2:
            running, query_handed = lax.optimization_barrier((running, query_handed))
        if step == hops - 2:
            running, own_handed = lax.optimization_barrier((running, own_handed))
    last_pairs = [
        (p * row_count + r, (p - 1) * row_count + r - 2)
        for p in range(1, pipe_count)
        for r in range(2, row_count)
    ]
    total = lax.ppermute(running, ("pipe", "row"), last_pairs) + own_handed
    key_handed = total[:, :key_width].astype(jnp.bfloat16)
    value_handed = total[:, key_width:].astype(jnp.bfloat16)
    return (query_handed[None], key_handed[None], value_handed[None], grad_handed[None])


def solution(mesh):
    in_specs = (
        P("pipe", "row", "col"),
        P("pipe", "col", "row"),
        P("pipe", "row", "col"),
        P("pipe", "row", "col"),
        P("pipe", "row", "col"),
        P("pipe", None),
        P("pipe", None),
    )
    out_specs = (
        P("pipe", "row", "col"),
        P("pipe", "row", "col"),
        P("pipe", "row", "col"),
        P("pipe", "row", "col"),
    )
    return jax.shard_map(
        per_device, mesh=mesh, in_specs=in_specs, out_specs=out_specs, check_vma=False
    )
```
